512 devices in a mesh: tm: 64 (over x, z), wafer: 8 (over y, core).
Axes of the slice: x: 4, y: 4, z: 16, core: 2. Of those that a mesh axis runs over, the one named last changes fastest.
Arguments:
- timestream: float32 [64, 64, 1024], P('tm', 'wafer'), may hold values from -6 to 6
- noise_weight: float32 [64, 64], P('tm', 'wafer'), may hold values from 0.3 to 5.4, as said below
- hit_slot: int32 [64, 64, 1024], P('tm', 'wafer'), may hold values from 0 to 3
- tile_pixel: int32 [64, 64, 1024], P('tm', 'wafer'), may hold values from 0 to 16368
- pol_angle: float32 [64, 64, 1024], P('tm', 'wafer'), may hold values from -3.140625 to 3.140625
- hit_tiles: int32 [64, 4], P('tm'), may hold values from 0 to 127, as said below
- sky_map: float32 [128, 3, 16384], P('tm'), may hold values from -6 to 6
- precond: float32 [128, 6, 16384], P('tm'), may hold values from -0.45 to 8, as said below
Outputs:
- new_map: float32 [128, 3, 16384], P('tm')
- new_residual: float32 [64, 64, 1024], P('tm', 'wafer')
The draws below stay inside these ranges and needn't reach their ends.
Inputs may be any that keep to these rules, and one draw needn't show every extreme that they name: `hit_tiles`: the tiles of block c are distinct and lie among the 6 tiles (c - 1) * 2 to (c + 2) * 2 - 1, taken modulo 128; the first lies among the lower 2 of them, the second among the upper 2. `noise_weight`: Positive. `precond`: at every pixel each diagonal entry exceeds the sum of the magnitudes of the off-diagonal entries of its row. `tile_pixel`: the last 15 pixels of every tile are never hit.
All inputs are finite; a program needn't handle non-finite values.
Results may differ from the reference program's by a relative error of at most 0.0003.
Values sent between devices are 32-bit elements; how exact they have to be, the bound alone decides.
No kernel may reach another device: no remote copies, remote signals or barrier semaphores. Data moves between devices by JAX's collectives and lax.ppermute only.
A program may use at most 64 MiB of HBM per device.

```python
import jax
import jax.numpy as jnp
from jax import lax

PIX = 16384
HITS = 4
TILE_DEV = 2
SAMP = 1024
BLOCKS = 64
DETS = 64
NT = 128


def draw_noise_weight(key, part):
    base = jnp.exp(jax.random.uniform(key, (BLOCKS, DETS), jnp.float32, jnp.log(0.4), jnp.log(1.6)))
    rising = 1.0 + 2.0 * jnp.arange(BLOCKS, dtype=jnp.float32) / (BLOCKS - 1)
    return (base * rising[:, None]).astype(jnp.float32)


def draw_precond(key, part):
    key_diag, key_off = jax.random.split(jax.random.fold_in(key, 7))
    diag = jnp.exp(jax.random.uniform(key_diag, (NT, 3, PIX), jnp.float32, 0.0, jnp.log(4.0)))
    off = jax.random.uniform(key_off, (NT, 3, PIX), jnp.float32, -0.4, 0.4)
    return jnp.concatenate([diag, off], axis=1)


def draw_hit_tiles(key, part):
    key_low, key_high, key_rest = jax.random.split(jax.random.fold_in(key, 11), 3)
    lower = jax.random.randint(key_low, (BLOCKS,), 0, TILE_DEV)
    upper = 2 * TILE_DEV + jax.random.randint(key_high, (BLOCKS,), 0, TILE_DEV)
    keys = jax.random.split(key_rest, BLOCKS)
    orders = jax.vmap(lambda single: jax.random.permutation(single, 3 * TILE_DEV - 2))(keys)[:, :HITS - 2]
    placed = orders + (orders >= lower[:, None]).astype(jnp.int32)
    placed = placed + (placed >= upper[:, None]).astype(jnp.int32)
    local = jnp.concatenate([lower[:, None], upper[:, None], placed], axis=1)
    block_ids = jnp.arange(BLOCKS, dtype=jnp.int32)
    return jnp.mod(local + (block_ids[:, None] - 1) * TILE_DEV, NT).astype(jnp.int32)


def touch_ends(entries, key, low, largest):
    extent = entries.shape
    index_at = [jax.random.randint(jax.random.fold_in(key, axis), (), 0, extent[axis]) for axis in range(len(extent))]
    entries = entries.at[tuple(index_at)].set(low)
    longest = extent.index(max(extent))
    index_at[longest] = (index_at[longest] + 1) % extent[longest]
    return entries.at[tuple(index_at)].set(largest)


def levels(own_key, extent, cuts, low, largest):
    loudness, own = 1.0, jax.random.fold_in(own_key, 6)
    for dim, shards_of in cuts:
        draws = jnp.exp(jax.random.uniform(jax.random.fold_in(own, dim), (shards_of,), jnp.float32, low / len(cuts), largest / len(cuts)))
        loudness = loudness * jnp.repeat(draws, extent[dim] // shards_of).reshape([-1 if axis == dim else 1 for axis in range(len(extent))])
    return loudness


def scatter_about(key, shape, width, reach, shards=(), kind=jnp.bfloat16):
    result = jax.random.normal(key, shape, jnp.float32) * width
    if len(shards) > 0:
        result = levels(key, shape, shards, -0.22, 0.18) * result
    return jnp.clip(result, min=-reach, max=reach).astype(kind)


def setup_inputs(seed: int = 0) -> dict:
    splits = jax.random.split(jax.random.key(seed), 9)
    timestream = scatter_about(splits[0], (BLOCKS, DETS, SAMP), 1.0, 6.0, ((0, 64), (1, 8)), jnp.float32)
    noise_weight = draw_noise_weight(jax.random.fold_in(splits[8], 71), 0)
    hit_slot = touch_ends(jax.random.randint(splits[2], (BLOCKS, DETS, SAMP), 0, HITS), jax.random.fold_in(splits[2], 1), 0, HITS - 1).astype(jnp.int32)
    tile_pixel = touch_ends(jax.random.randint(splits[3], (BLOCKS, DETS, SAMP), 0, PIX - 15), jax.random.fold_in(splits[3], 1), 0, (PIX - 15) - 1).astype(jnp.int32)
    pol_angle = jnp.clip(jax.random.uniform(splits[4], (BLOCKS, DETS, SAMP), jnp.float32, -3.140625, 3.140625), -3.140625, 3.140625)
    hit_tiles = draw_hit_tiles(jax.random.fold_in(splits[8], 71), 0)
    sky_map = scatter_about(splits[6], (NT, 3, PIX), 1.0, 6.0, ((0, 64),), jnp.float32)
    precond = draw_precond(jax.random.fold_in(splits[8], 71), 0)
    return dict(timestream=timestream, noise_weight=noise_weight, hit_slot=hit_slot, tile_pixel=tile_pixel, pol_angle=pol_angle, hit_tiles=hit_tiles, sky_map=sky_map, precond=precond)


def precondition(gradient, inverse):
    g_i = gradient[:, 0]
    g_q = gradient[:, 1]
    g_u = gradient[:, 2]
    out_i = inverse[:, 0] * g_i + inverse[:, 3] * g_q + inverse[:, 4] * g_u
    out_q = inverse[:, 3] * g_i + inverse[:, 1] * g_q + inverse[:, 5] * g_u
    out_u = inverse[:, 4] * g_i + inverse[:, 5] * g_q + inverse[:, 2] * g_u
    return jnp.stack([out_i, out_q, out_u], axis=1)


def sampled_signal(map_rows, flat_index, cos_two, sin_two):
    sampled = jnp.take(map_rows, flat_index, axis=1)
    return sampled[0] + cos_two * sampled[1] + sin_two * sampled[2]


def reference(timestream, noise_weight, hit_slot, tile_pixel, pol_angle, hit_tiles, sky_map, precond):
    map_rows = jnp.transpose(sky_map, (1, 0, 2)).reshape(3, NT * PIX)
    block_ids = jnp.arange(BLOCKS, dtype=jnp.int32)

    def pointing(block):
        flat_index = (hit_tiles[block][hit_slot[block]] * PIX + tile_pixel[block]).astype(jnp.int32)
        doubled = 2.0 * pol_angle[block]
        return flat_index, jnp.cos(doubled), jnp.sin(doubled)

    def bin_block(binned, block):
        flat_index, cos_two, sin_two = pointing(block)
        resid = timestream[block] - sampled_signal(map_rows, flat_index, cos_two, sin_two)
        weighted = noise_weight[block][:, None] * resid
        terms = jnp.stack([weighted, weighted * cos_two, weighted * sin_two]).reshape(3, -1)
        return binned.at[:, flat_index.reshape(-1)].add(terms), None

    binned, _ = lax.scan(bin_block, jnp.zeros((3, NT * PIX), jnp.float32), block_ids)
    gradient = jnp.transpose(binned.reshape(3, NT, PIX), (1, 0, 2))
    direction = precondition(gradient, precond)
    slope = jnp.sum(gradient * direction)
    dir_rows = jnp.transpose(direction, (1, 0, 2)).reshape(3, NT * PIX)

    def curve_block(total, block):
        flat_index, cos_two, sin_two = pointing(block)
        rescanned = sampled_signal(dir_rows, flat_index, cos_two, sin_two)
        return total + jnp.sum(noise_weight[block][:, None] * rescanned * rescanned), None

    curvature, _ = lax.scan(curve_block, jnp.zeros((), jnp.float32), block_ids)
    step_size = slope / curvature
    new_map = sky_map + step_size * direction

    def residual_block(block):
        flat_index, cos_two, sin_two = pointing(block)
        resid = timestream[block] - sampled_signal(map_rows, flat_index, cos_two, sin_two)
        return resid - step_size * sampled_signal(dir_rows, flat_index, cos_two, sin_two)

    new_residual = lax.map(residual_block, block_ids)
    return new_map, new_residual
```

```python
import functools

import jax
import jax.numpy as jnp
from jax import lax
from jax.experimental import pallas as pl
from jax.experimental.pallas import tpu as pltpu
from jax.sharding import Mesh
from jax.sharding import PartitionSpec as P

TM = ("tm_0", "tm_1")
WAFER = ("wafer_0", "wafer_1")
TM_WAFER = ("tm_0", "tm_1", "wafer_0", "wafer_1")


def with_halo(block, sides, width):
    for axis, dim in sides:
        count = lax.axis_size(axis)
        forward = [(i, i + 1) for i in range(count - 1)]
        forward.append((count - 1, 0))
        backward = [(target, source) for source, target in forward]
        low = lax.ppermute(
            lax.slice_in_dim(block, block.shape[dim] - width, None, axis=dim), axis, forward
        )
        high = lax.ppermute(lax.slice_in_dim(block, 0, width, axis=dim), axis, backward)
        block = jnp.concatenate([low, block, high], axis=dim)
    return block


def passed_along(value, axis, by):
    count = lax.axis_size(axis)
    return lax.ppermute(value, axis, [(i, (i + by) % count) for i in range(count)])


def in_blocks(value, dim, count):
    shape = value.shape
    parts = value.reshape(*shape[:dim], count, shape[dim] // count, *shape[dim + 1 :])
    return jnp.moveaxis(parts, dim, 0)


def sum_at_owner(value, axis, dim):
    count = lax.axis_size(axis)
    parts = lax.all_to_all(in_blocks(value, dim, count), axis, 0, 0, tiled=True)
    return jnp.sum(parts, axis=0)


def laid_out(parts, dim):
    shape = list(parts.shape[1:])
    shape[dim] *= parts.shape[0]
    return jnp.moveaxis(parts, 0, dim).reshape(shape)


def copy_for_each(value, axis):
    copies = jnp.broadcast_to(value, (lax.axis_size(axis), *value.shape))
    return lax.all_to_all(copies, axis, split_axis=0, concat_axis=0, tiled=True)


def collect(value, axis, dim):
    return laid_out(copy_for_each(value, axis), dim)


def by_axis(value, axes):
    return functools.reduce(lax.psum, axes, value)


def precondition(gradient, inverse):
    g_i = gradient[:, 0]
    g_q = gradient[:, 1]
    g_u = gradient[:, 2]
    out_i = inverse[:, 0] * g_i + inverse[:, 3] * g_q + inverse[:, 4] * g_u
    out_q = inverse[:, 3] * g_i + inverse[:, 1] * g_q + inverse[:, 5] * g_u
    out_u = inverse[:, 4] * g_i + inverse[:, 5] * g_q + inverse[:, 2] * g_u
    return jnp.stack([out_i, out_q, out_u], axis=1)


SIDE = 128


def split3(value):
    hi = value.astype(jnp.bfloat16)
    rest = value - hi.astype(jnp.float32)
    mid = rest.astype(jnp.bfloat16)
    lo = (rest - mid.astype(jnp.float32)).astype(jnp.bfloat16)
    return hi, mid, lo


def row_onehot(slot, pix, rows):
    row = slot * SIDE + jnp.right_shift(pix, 7)
    ids = lax.broadcasted_iota(jnp.int32, (rows, pix.shape[1]), 0)
    return (ids == row).astype(jnp.bfloat16)


def col_mask(pix):
    col = jnp.bitwise_and(pix, SIDE - 1)
    ids = lax.broadcasted_iota(jnp.int32, (SIDE, pix.shape[1]), 0)
    return ids == col


def sample_map(pieces, at, mask, comp):
    picked = None
    for piece in pieces:
        part = jnp.dot(piece[comp], at, preferred_element_type=jnp.float32)
        picked = part if picked is None else picked + part
    return jnp.sum(jnp.where(mask, picked, 0.0), axis=0, keepdims=True)


def bin_kernel(w_ref, mt_ref, slot_ref, pix_ref, cos_ref, sin_ref, ts_ref, resid_ref, g_ref,
               hi_ref, mid_ref, lo_ref, acc_ref):
    hi, mid, lo = split3(mt_ref[...])
    hi_ref[...] = hi
    mid_ref[...] = mid
    lo_ref[...] = lo
    acc_ref[...] = jnp.zeros(acc_ref.shape, jnp.float32)
    rows = mt_ref.shape[2]
    nt = (((1,), (1,)), ((), ()))

    def body(d, carry):
        slot = slot_ref[pl.ds(d, 1), :]
        pix = pix_ref[pl.ds(d, 1), :]
        cs = cos_ref[pl.ds(d, 1), :]
        sn = sin_ref[pl.ds(d, 1), :]
        at = row_onehot(slot, pix, rows)
        mask = col_mask(pix)
        pieces = (hi_ref, mid_ref, lo_ref)
        v0 = sample_map(pieces, at, mask, 0)
        v1 = sample_map(pieces, at, mask, 1)
        v2 = sample_map(pieces, at, mask, 2)
        resid = ts_ref[pl.ds(d, 1), :] - (v0 + cs * v1 + sn * v2)
        resid_ref[pl.ds(d, 1), :] = resid
        weighted = w_ref[d] * resid
        for comp, term in ((0, weighted), (1, weighted * cs), (2, weighted * sn)):
            dt = jnp.where(mask, term, 0.0)
            total = None
            for piece in split3(dt):
                part = lax.dot_general(at, piece, nt, preferred_element_type=jnp.float32)
                total = part if total is None else total + part
            acc_ref[comp] += total
        return carry

    lax.fori_loop(0, slot_ref.shape[0], body, 0)
    for s in range(g_ref.shape[0]):
        for comp in range(3):
            g_ref[s, comp] = acc_ref[comp, s * SIDE:(s + 1) * SIDE, :]


def scan_kernel(mt_ref, slot_ref, pix_ref, cos_ref, sin_ref, out_ref, hi_ref, mid_ref, lo_ref):
    hi, mid, lo = split3(mt_ref[...])
    hi_ref[...] = hi
    mid_ref[...] = mid
    lo_ref[...] = lo
    rows = mt_ref.shape[2]

    def body(d, carry):
        slot = slot_ref[pl.ds(d, 1), :]
        pix = pix_ref[pl.ds(d, 1), :]
        at = row_onehot(slot, pix, rows)
        mask = col_mask(pix)
        pieces = (hi_ref, mid_ref, lo_ref)
        v0 = sample_map(pieces, at, mask, 0)
        v1 = sample_map(pieces, at, mask, 1)
        v2 = sample_map(pieces, at, mask, 2)
        out_ref[pl.ds(d, 1), :] = v0 + cos_ref[pl.ds(d, 1), :] * v1 + sin_ref[pl.ds(d, 1), :] * v2
        return carry

    lax.fori_loop(0, slot_ref.shape[0], body, 0)


def transposed_window(window, local_ids):
    hits = jnp.take(window, local_ids, axis=0)
    count = hits.shape[0]
    grid = hits.reshape(count, 3, SIDE, SIDE)
    return jnp.transpose(grid, (1, 3, 0, 2)).reshape(3, SIDE, count * SIDE)


VMEM = pltpu.MemorySpace.VMEM


def bin_call(weights, mt, slot, pix, cos_two, sin_two, ts):
    dets, samp = slot.shape
    hits = mt.shape[2] // SIDE
    smem = pl.BlockSpec(memory_space=pltpu.SMEM)
    vmem = pl.BlockSpec(memory_space=VMEM)
    return pl.pallas_call(
        bin_kernel,
        out_shape=(
            jax.ShapeDtypeStruct((dets, samp), jnp.float32),
            jax.ShapeDtypeStruct((hits, 3, SIDE, SIDE), jnp.float32),
        ),
        in_specs=[smem] + [vmem] * 6,
        out_specs=(vmem, vmem),
        scratch_shapes=[pltpu.VMEM(mt.shape, jnp.bfloat16)] * 3
        + [pltpu.VMEM((3, hits * SIDE, SIDE), jnp.float32)],
    )(weights, mt, slot, pix, cos_two, sin_two, ts)


def scan_call(mt, slot, pix, cos_two, sin_two):
    vmem = pl.BlockSpec(memory_space=VMEM)
    return pl.pallas_call(
        scan_kernel,
        out_shape=jax.ShapeDtypeStruct(slot.shape, jnp.float32),
        in_specs=[vmem] * 5,
        out_specs=vmem,
        scratch_shapes=[pltpu.VMEM(mt.shape, jnp.bfloat16)] * 3,
    )(mt, slot, pix, cos_two, sin_two)


def local(timestream, noise_weight, hit_slot, tile_pixel, pol_angle, hit_tiles, sky_map, precond):
    tiles_dev = sky_map.shape[0]
    pixels = sky_map.shape[2]
    all_tiles = tiles_dev * lax.axis_size(TM)
    position = lax.axis_index(TM)
    local_ids = jnp.mod(hit_tiles[0] - (position - 1) * tiles_dev, all_tiles)
    doubled = 2.0 * pol_angle[0]
    cos_two = jnp.cos(doubled)
    sin_two = jnp.sin(doubled)
    weights = noise_weight[0]
    slot = hit_slot[0]
    pix = tile_pixel[0]
    window = with_halo(sky_map, ((TM, 0),), tiles_dev)
    mt = transposed_window(window, local_ids)
    resid, binned = bin_call(weights, mt, slot, pix, cos_two, sin_two, timestream[0])
    partial_tiles = binned.reshape(binned.shape[0], 3, pixels)
    near_tiles = jnp.zeros((3 * tiles_dev, 3, pixels), jnp.float32).at[local_ids].add(partial_tiles)
    from_upper = passed_along(near_tiles[:tiles_dev], TM, -1)
    from_lower = passed_along(near_tiles[2 * tiles_dev :], TM, 1)
    owned_tiles = near_tiles[tiles_dev : 2 * tiles_dev] + from_upper + from_lower
    grad_share = sum_at_owner(owned_tiles, WAFER, 2)
    share_width = grad_share.shape[2]
    inverse_share = lax.dynamic_slice_in_dim(
        precond, lax.axis_index(WAFER) * share_width, share_width, 2
    )
    dir_share = precondition(grad_share, inverse_share)
    slope_part = jnp.sum(grad_share * dir_share)
    direction = collect(dir_share, WAFER, 2)
    dir_window = with_halo(direction, ((TM, 0),), tiles_dev)
    dir_mt = transposed_window(dir_window, local_ids)
    rescanned = scan_call(dir_mt, slot, pix, cos_two, sin_two)
    curve_part = jnp.sum(weights[:, None] * rescanned * rescanned)
    totals = lax.psum(jnp.stack([slope_part, curve_part]), TM_WAFER)
    step_size = totals[0] / totals[1]
    new_map = sky_map + step_size * direction
    new_residual = (resid - step_size * rescanned)[None]
    return (new_map, new_residual)


def solution(mesh):
    split = Mesh(mesh.devices.reshape(4, 16, 4, 2), ("tm_0", "tm_1", "wafer_0", "wafer_1"))
    in_specs = (
        P(TM, WAFER, None),
        P(TM, WAFER),
        P(TM, WAFER, None),
        P(TM, WAFER, None),
        P(TM, WAFER, None),
        P(TM, None),
        P(TM, None, None),
        P(TM, None, None),
    )
    out_specs = (P(TM, None, None), P(TM, WAFER, None))
    return jax.shard_map(local, mesh=split, in_specs=in_specs, out_specs=out_specs, check_vma=False)
```

```python
import functools

import jax
import jax.numpy as jnp
from jax import lax
from jax.experimental import pallas as pl
from jax.experimental.pallas import tpu as pltpu
from jax.sharding import Mesh
from jax.sharding import PartitionSpec as P

TM = ("tm_0", "tm_1")
WAFER = ("wafer_0", "wafer_1")
TM_WAFER = ("tm_0", "tm_1", "wafer_0", "wafer_1")


def with_halo(block, sides, width):
    for axis, dim in sides:
        count = lax.axis_size(axis)
        forward = [(i, i + 1) for i in range(count - 1)]
        forward.append((count - 1, 0))
        backward = [(target, source) for source, target in forward]
        low = lax.ppermute(
            lax.slice_in_dim(block, block.shape[dim] - width, None, axis=dim), axis, forward
        )
        high = lax.ppermute(lax.slice_in_dim(block, 0, width, axis=dim), axis, backward)
        block = jnp.concatenate([low, block, high], axis=dim)
    return block


def passed_along(value, axis, by):
    count = lax.axis_size(axis)
    return lax.ppermute(value, axis, [(i, (i + by) % count) for i in range(count)])


def in_blocks(value, dim, count):
    shape = value.shape
    parts = value.reshape(*shape[:dim], count, shape[dim] // count, *shape[dim + 1 :])
    return jnp.moveaxis(parts, dim, 0)


def sum_at_owner(value, axis, dim):
    count = lax.axis_size(axis)
    parts = lax.all_to_all(in_blocks(value, dim, count), axis, 0, 0, tiled=True)
    return jnp.sum(parts, axis=0)


def laid_out(parts, dim):
    shape = list(parts.shape[1:])
    shape[dim] *= parts.shape[0]
    return jnp.moveaxis(parts, 0, dim).reshape(shape)


def copy_for_each(value, axis):
    copies = jnp.broadcast_to(value, (lax.axis_size(axis), *value.shape))
    return lax.all_to_all(copies, axis, split_axis=0, concat_axis=0, tiled=True)


def collect(value, axis, dim):
    return laid_out(copy_for_each(value, axis), dim)


def by_axis(value, axes):
    return functools.reduce(lax.psum, axes, value)


def precondition(gradient, inverse):
    g_i = gradient[:, 0]
    g_q = gradient[:, 1]
    g_u = gradient[:, 2]
    out_i = inverse[:, 0] * g_i + inverse[:, 3] * g_q + inverse[:, 4] * g_u
    out_q = inverse[:, 3] * g_i + inverse[:, 1] * g_q + inverse[:, 5] * g_u
    out_u = inverse[:, 4] * g_i + inverse[:, 5] * g_q + inverse[:, 2] * g_u
    return jnp.stack([out_i, out_q, out_u], axis=1)


SIDE = 128


def split3(value):
    hi = value.astype(jnp.bfloat16)
    rest = value - hi.astype(jnp.float32)
    mid = rest.astype(jnp.bfloat16)
    lo = (rest - mid.astype(jnp.float32)).astype(jnp.bfloat16)
    return hi, mid, lo


def row_onehot(slot, pix, rows):
    row = slot * SIDE + jnp.right_shift(pix, 7)
    ids = lax.broadcasted_iota(jnp.int32, (rows, pix.shape[1]), 0)
    return (ids == row).astype(jnp.bfloat16)


def col_mask(pix):
    col = jnp.bitwise_and(pix, SIDE - 1)
    ids = lax.broadcasted_iota(jnp.int32, (SIDE, pix.shape[1]), 0)
    return ids == col


def sample_map(pieces, at, mask, comp):
    picked = None
    for piece in pieces:
        part = jnp.dot(piece[comp], at, preferred_element_type=jnp.float32)
        picked = part if picked is None else picked + part
    return jnp.sum(jnp.where(mask, picked, 0.0), axis=0, keepdims=True)


def bin_kernel(w_ref, mt_ref, slot_ref, pix_ref, cos_ref, sin_ref, ts_ref, resid_ref, g_ref,
               hi_ref, mid_ref, lo_ref, acc_ref):
    hi, mid, lo = split3(mt_ref[...])
    hi_ref[...] = hi
    mid_ref[...] = mid
    lo_ref[...] = lo
    acc_ref[...] = jnp.zeros(acc_ref.shape, jnp.float32)
    rows = mt_ref.shape[2]
    nt = (((1,), (1,)), ((), ()))

    def body(d, carry):
        slot = slot_ref[pl.ds(d, 1), :]
        pix = pix_ref[pl.ds(d, 1), :]
        cs = cos_ref[pl.ds(d, 1), :]
        sn = sin_ref[pl.ds(d, 1), :]
        at = row_onehot(slot, pix, rows)
        mask = col_mask(pix)
        pieces = (hi_ref, mid_ref, lo_ref)
        v0 = sample_map(pieces, at, mask, 0)
        v1 = sample_map(pieces, at, mask, 1)
        v2 = sample_map(pieces, at, mask, 2)
        resid = ts_ref[pl.ds(d, 1), :] - (v0 + cs * v1 + sn * v2)
        resid_ref[pl.ds(d, 1), :] = resid
        weighted = w_ref[d] * resid
        for comp, term in ((0, weighted), (1, weighted * cs), (2, weighted * sn)):
            dt = jnp.where(mask, term, 0.0)
            total = None
            for piece in split3(dt):
                part = lax.dot_general(at, piece, nt, preferred_element_type=jnp.float32)
                total = part if total is None else total + part
            acc_ref[comp] += total
        return carry

    lax.fori_loop(0, slot_ref.shape[0], body, 0)
    for s in range(g_ref.shape[0]):
        for comp in range(3):
            g_ref[s, comp] = acc_ref[comp, s * SIDE:(s + 1) * SIDE, :]


def scan_kernel(mt_ref, slot_ref, pix_ref, cos_ref, sin_ref, out_ref, hi_ref, mid_ref, lo_ref):
    hi, mid, lo = split3(mt_ref[...])
    hi_ref[...] = hi
    mid_ref[...] = mid
    lo_ref[...] = lo
    rows = mt_ref.shape[2]

    def body(d, carry):
        slot = slot_ref[pl.ds(d, 1), :]
        pix = pix_ref[pl.ds(d, 1), :]
        at = row_onehot(slot, pix, rows)
        mask = col_mask(pix)
        pieces = (hi_ref, mid_ref, lo_ref)
        v0 = sample_map(pieces, at, mask, 0)
        v1 = sample_map(pieces, at, mask, 1)
        v2 = sample_map(pieces, at, mask, 2)
        out_ref[pl.ds(d, 1), :] = v0 + cos_ref[pl.ds(d, 1), :] * v1 + sin_ref[pl.ds(d, 1), :] * v2
        return carry

    lax.fori_loop(0, slot_ref.shape[0], body, 0)


def transposed_window(window, local_ids):
    hits = jnp.take(window, local_ids, axis=0)
    count = hits.shape[0]
    grid = hits.reshape(count, 3, SIDE, SIDE)
    return jnp.transpose(grid, (1, 3, 0, 2)).reshape(3, SIDE, count * SIDE)


VMEM = pltpu.MemorySpace.VMEM


def bin_call(weights, mt, slot, pix, cos_two, sin_two, ts):
    dets, samp = slot.shape
    hits = mt.shape[2] // SIDE
    smem = pl.BlockSpec(memory_space=pltpu.SMEM)
    vmem = pl.BlockSpec(memory_space=VMEM)
    return pl.pallas_call(
        bin_kernel,
        out_shape=(
            jax.ShapeDtypeStruct((dets, samp), jnp.float32),
            jax.ShapeDtypeStruct((hits, 3, SIDE, SIDE), jnp.float32),
        ),
        in_specs=[smem] + [vmem] * 6,
        out_specs=(vmem, vmem),
        scratch_shapes=[pltpu.VMEM(mt.shape, jnp.bfloat16)] * 3
        + [pltpu.VMEM((3, hits * SIDE, SIDE), jnp.float32)],
    )(weights, mt, slot, pix, cos_two, sin_two, ts)


def scan_call(mt, slot, pix, cos_two, sin_two):
    vmem = pl.BlockSpec(memory_space=VMEM)
    return pl.pallas_call(
        scan_kernel,
        out_shape=jax.ShapeDtypeStruct(slot.shape, jnp.float32),
        in_specs=[vmem] * 5,
        out_specs=vmem,
        scratch_shapes=[pltpu.VMEM(mt.shape, jnp.bfloat16)] * 3,
    )(mt, slot, pix, cos_two, sin_two)


def local(timestream, noise_weight, hit_slot, tile_pixel, pol_angle, hit_tiles, sky_map, precond):
    tiles_dev = sky_map.shape[0]
    pixels = sky_map.shape[2]
    all_tiles = tiles_dev * lax.axis_size(TM)
    position = lax.axis_index(TM)
    local_ids = jnp.mod(hit_tiles[0] - (position - 1) * tiles_dev, all_tiles)
    doubled = 2.0 * pol_angle[0]
    cos_two = jnp.cos(doubled)
    sin_two = jnp.sin(doubled)
    weights = noise_weight[0]
    slot = hit_slot[0]
    pix = tile_pixel[0]
    window = with_halo(sky_map, ((TM, 0),), tiles_dev)
    mt = transposed_window(window, local_ids)
    resid, binned = bin_call(weights, mt, slot, pix, cos_two, sin_two, timestream[0])
    partial_tiles = binned.reshape(binned.shape[0], 3, pixels)
    near_tiles = jnp.zeros((3 * tiles_dev, 3, pixels), jnp.float32).at[local_ids].add(partial_tiles)
    from_upper = passed_along(near_tiles[:tiles_dev], TM, -1)
    from_lower = passed_along(near_tiles[2 * tiles_dev :], TM, 1)
    owned_tiles = near_tiles[tiles_dev : 2 * tiles_dev] + from_upper + from_lower
    grad_share = sum_at_owner(owned_tiles, WAFER, 2)
    share_width = grad_share.shape[2]
    inverse_share = lax.dynamic_slice_in_dim(
        precond, lax.axis_index(WAFER) * share_width, share_width, 2
    )
    dir_share = precondition(grad_share, inverse_share)
    slope_part = jnp.sum(grad_share * dir_share)
    direction = collect(dir_share, WAFER, 2)
    dir_window = with_halo(direction, ((TM, 0),), tiles_dev)
    dir_mt = transposed_window(dir_window, local_ids)
    rescanned = scan_call(dir_mt, slot, pix, cos_two, sin_two)
    curve_part = jnp.sum(weights[:, None] * rescanned * rescanned)
    totals = by_axis(jnp.stack([slope_part, curve_part]), ("wafer_1", "wafer_0", "tm_0", "tm_1"))
    step_size = totals[0] / totals[1]
    new_map = sky_map + step_size * direction
    new_residual = (resid - step_size * rescanned)[None]
    return (new_map, new_residual)


def solution(mesh):
    split = Mesh(mesh.devices.reshape(4, 16, 4, 2), ("tm_0", "tm_1", "wafer_0", "wafer_1"))
    in_specs = (
        P(TM, WAFER, None),
        P(TM, WAFER),
        P(TM, WAFER, None),
        P(TM, WAFER, None),
        P(TM, WAFER, None),
        P(TM, None),
        P(TM, None, None),
        P(TM, None, None),
    )
    out_specs = (P(TM, None, None), P(TM, WAFER, None))
    return jax.shard_map(local, mesh=split, in_specs=in_specs, out_specs=out_specs, check_vma=False)
```

```python
import functools

import jax
import jax.numpy as jnp
from jax import lax
from jax.experimental import pallas as pl
from jax.experimental.pallas import tpu as pltpu
from jax.sharding import Mesh
from jax.sharding import PartitionSpec as P

TM = ("tm_0", "tm_hi", "tm_lo")
WAFER = ("wafer_0", "wafer_1")
TM_WAFER = ("tm_0", "tm_hi", "tm_lo", "wafer_0", "wafer_1")


def with_halo(block, sides, width):
    for axis, dim in sides:
        count = lax.axis_size(axis)
        forward = [(i, i + 1) for i in range(count - 1)]
        forward.append((count - 1, 0))
        backward = [(target, source) for source, target in forward]
        low = lax.ppermute(
            lax.slice_in_dim(block, block.shape[dim] - width, None, axis=dim), axis, forward
        )
        high = lax.ppermute(lax.slice_in_dim(block, 0, width, axis=dim), axis, backward)
        block = jnp.concatenate([low, block, high], axis=dim)
    return block


def passed_along(value, axis, by):
    count = lax.axis_size(axis)
    return lax.ppermute(value, axis, [(i, (i + by) % count) for i in range(count)])


def in_blocks(value, dim, count):
    shape = value.shape
    parts = value.reshape(*shape[:dim], count, shape[dim] // count, *shape[dim + 1 :])
    return jnp.moveaxis(parts, dim, 0)


def sum_at_owner(value, axis, dim):
    count = lax.axis_size(axis)
    parts = lax.all_to_all(in_blocks(value, dim, count), axis, 0, 0, tiled=True)
    return jnp.sum(parts, axis=0)


def laid_out(parts, dim):
    shape = list(parts.shape[1:])
    shape[dim] *= parts.shape[0]
    return jnp.moveaxis(parts, 0, dim).reshape(shape)


def copy_for_each(value, axis):
    copies = jnp.broadcast_to(value, (lax.axis_size(axis), *value.shape))
    return lax.all_to_all(copies, axis, split_axis=0, concat_axis=0, tiled=True)


def collect(value, axis, dim):
    return laid_out(copy_for_each(value, axis), dim)


def by_axis(value, axes):
    return functools.reduce(lax.psum, axes, value)


def precondition(gradient, inverse):
    g_i = gradient[:, 0]
    g_q = gradient[:, 1]
    g_u = gradient[:, 2]
    out_i = inverse[:, 0] * g_i + inverse[:, 3] * g_q + inverse[:, 4] * g_u
    out_q = inverse[:, 3] * g_i + inverse[:, 1] * g_q + inverse[:, 5] * g_u
    out_u = inverse[:, 4] * g_i + inverse[:, 5] * g_q + inverse[:, 2] * g_u
    return jnp.stack([out_i, out_q, out_u], axis=1)


SIDE = 128


def split2(value):
    hi = value.astype(jnp.bfloat16)
    lo = (value - hi.astype(jnp.float32)).astype(jnp.bfloat16)
    return hi, lo


def row_onehot(slot, pix, rows):
    row = slot * SIDE + jnp.right_shift(pix, 7)
    ids = lax.broadcasted_iota(jnp.int32, (rows, pix.shape[1]), 0)
    return (ids == row).astype(jnp.bfloat16)


def col_mask(pix):
    col = jnp.bitwise_and(pix, SIDE - 1)
    ids = lax.broadcasted_iota(jnp.int32, (SIDE, pix.shape[1]), 0)
    return ids == col


def stacked_map(mt_ref, lhs_ref):
    hi, lo = split2(mt_ref[...])
    for comp in range(3):
        lhs_ref[comp * SIDE:(comp + 1) * SIDE, :] = hi[comp]
        lhs_ref[(3 + comp) * SIDE:(4 + comp) * SIDE, :] = lo[comp]


def sampled(lhs_ref, at, mask):
    both = jnp.dot(lhs_ref[...], at, preferred_element_type=jnp.float32)
    values = []
    for comp in range(3):
        full = both[comp * SIDE:(comp + 1) * SIDE] + both[(3 + comp) * SIDE:(4 + comp) * SIDE]
        values.append(jnp.sum(jnp.where(mask, full, 0.0), axis=0, keepdims=True))
    return values


def bin_kernel(w_ref, mt_ref, slot_ref, pix_ref, cos_ref, sin_ref, ts_ref, resid_ref, g_ref,
               lhs_ref, rhs_ref, acc_ref):
    stacked_map(mt_ref, lhs_ref)
    acc_ref[...] = jnp.zeros(acc_ref.shape, jnp.float32)
    rows = mt_ref.shape[2]
    nt = (((1,), (1,)), ((), ()))

    def body(d, carry):
        slot = slot_ref[pl.ds(d, 1), :]
        pix = pix_ref[pl.ds(d, 1), :]
        cs = cos_ref[pl.ds(d, 1), :]
        sn = sin_ref[pl.ds(d, 1), :]
        at = row_onehot(slot, pix, rows)
        mask = col_mask(pix)
        v0, v1, v2 = sampled(lhs_ref, at, mask)
        resid = ts_ref[pl.ds(d, 1), :] - (v0 + cs * v1 + sn * v2)
        resid_ref[pl.ds(d, 1), :] = resid
        weighted = w_ref[d] * resid
        for comp, term in ((0, weighted), (1, weighted * cs), (2, weighted * sn)):
            hi, lo = split2(jnp.where(mask, term, 0.0))
            rhs_ref[comp * SIDE:(comp + 1) * SIDE, :] = hi
            rhs_ref[(3 + comp) * SIDE:(4 + comp) * SIDE, :] = lo
        acc_ref[...] += lax.dot_general(at, rhs_ref[...], nt, preferred_element_type=jnp.float32)
        return carry

    lax.fori_loop(0, slot_ref.shape[0], body, 0)
    for s in range(g_ref.shape[0]):
        for comp in range(3):
            rows_s = slice(s * SIDE, (s + 1) * SIDE)
            g_ref[s, comp] = (acc_ref[rows_s, comp * SIDE:(comp + 1) * SIDE]
                              + acc_ref[rows_s, (3 + comp) * SIDE:(4 + comp) * SIDE])


def scan_kernel(mt_ref, slot_ref, pix_ref, cos_ref, sin_ref, out_ref, lhs_ref):
    stacked_map(mt_ref, lhs_ref)
    rows = mt_ref.shape[2]

    def body(d, carry):
        slot = slot_ref[pl.ds(d, 1), :]
        pix = pix_ref[pl.ds(d, 1), :]
        at = row_onehot(slot, pix, rows)
        mask = col_mask(pix)
        v0, v1, v2 = sampled(lhs_ref, at, mask)
        out_ref[pl.ds(d, 1), :] = v0 + cos_ref[pl.ds(d, 1), :] * v1 + sin_ref[pl.ds(d, 1), :] * v2
        return carry

    lax.fori_loop(0, slot_ref.shape[0], body, 0)


def transposed_window(window, local_ids):
    hits = jnp.take(window, local_ids, axis=0)
    count = hits.shape[0]
    grid = hits.reshape(count, 3, SIDE, SIDE)
    return jnp.transpose(grid, (1, 3, 0, 2)).reshape(3, SIDE, count * SIDE)


VMEM = pltpu.MemorySpace.VMEM


def bin_call(weights, mt, slot, pix, cos_two, sin_two, ts):
    dets, samp = slot.shape
    hits = mt.shape[2] // SIDE
    smem = pl.BlockSpec(memory_space=pltpu.SMEM)
    vmem = pl.BlockSpec(memory_space=VMEM)
    return pl.pallas_call(
        bin_kernel,
        out_shape=(
            jax.ShapeDtypeStruct((dets, samp), jnp.float32),
            jax.ShapeDtypeStruct((hits, 3, SIDE, SIDE), jnp.float32),
        ),
        in_specs=[smem] + [vmem] * 6,
        out_specs=(vmem, vmem),
        scratch_shapes=[
            pltpu.VMEM((6 * SIDE, hits * SIDE), jnp.bfloat16),
            pltpu.VMEM((6 * SIDE, samp), jnp.bfloat16),
            pltpu.VMEM((hits * SIDE, 6 * SIDE), jnp.float32),
        ],
    )(weights, mt, slot, pix, cos_two, sin_two, ts)


def scan_call(mt, slot, pix, cos_two, sin_two):
    vmem = pl.BlockSpec(memory_space=VMEM)
    return pl.pallas_call(
        scan_kernel,
        out_shape=jax.ShapeDtypeStruct(slot.shape, jnp.float32),
        in_specs=[vmem] * 5,
        out_specs=vmem,
        scratch_shapes=[pltpu.VMEM((6 * SIDE, mt.shape[2]), jnp.bfloat16)],
    )(mt, slot, pix, cos_two, sin_two)


def local(timestream, noise_weight, hit_slot, tile_pixel, pol_angle, hit_tiles, sky_map, precond):
    tiles_dev = sky_map.shape[0]
    pixels = sky_map.shape[2]
    all_tiles = tiles_dev * lax.axis_size(TM)
    position = lax.axis_index(TM)
    local_ids = jnp.mod(hit_tiles[0] - (position - 1) * tiles_dev, all_tiles)
    doubled = 2.0 * pol_angle[0]
    cos_two = jnp.cos(doubled)
    sin_two = jnp.sin(doubled)
    weights = noise_weight[0]
    slot = hit_slot[0]
    pix = tile_pixel[0]
    window = with_halo(sky_map, ((TM, 0),), tiles_dev)
    mt = transposed_window(window, local_ids)
    resid, binned = bin_call(weights, mt, slot, pix, cos_two, sin_two, timestream[0])
    partial_tiles = binned.reshape(binned.shape[0], 3, pixels)
    near_tiles = jnp.zeros((3 * tiles_dev, 3, pixels), jnp.float32).at[local_ids].add(partial_tiles)
    from_upper = passed_along(near_tiles[:tiles_dev], TM, -1)
    from_lower = passed_along(near_tiles[2 * tiles_dev :], TM, 1)
    owned_tiles = near_tiles[tiles_dev : 2 * tiles_dev] + from_upper + from_lower
    grad_share = sum_at_owner(owned_tiles, WAFER, 2)
    share_width = grad_share.shape[2]
    inverse_share = lax.dynamic_slice_in_dim(
        precond, lax.axis_index(WAFER) * share_width, share_width, 2
    )
    dir_share = precondition(grad_share, inverse_share)
    slope_part = jnp.sum(grad_share * dir_share)
    direction = collect(dir_share, WAFER, 2)
    dir_window = with_halo(direction, ((TM, 0),), tiles_dev)
    dir_mt = transposed_window(dir_window, local_ids)
    rescanned = scan_call(dir_mt, slot, pix, cos_two, sin_two)
    curve_part = jnp.sum(weights[:, None] * rescanned * rescanned)
    totals = by_axis(jnp.stack([slope_part, curve_part]), ("wafer_1", "wafer_0", "tm_0", "tm_lo", "tm_hi"))
    step_size = totals[0] / totals[1]
    new_map = sky_map + step_size * direction
    new_residual = (resid - step_size * rescanned)[None]
    return (new_map, new_residual)


def solution(mesh):
    split = Mesh(mesh.devices.reshape(4, 4, 4, 4, 2), TM_WAFER)
    in_specs = (
        P(TM, WAFER, None),
        P(TM, WAFER),
        P(TM, WAFER, None),
        P(TM, WAFER, None),
        P(TM, WAFER, None),
        P(TM, None),
        P(TM, None, None),
        P(TM, None, None),
    )
    out_specs = (P(TM, None, None), P(TM, WAFER, None))
    return jax.shard_map(local, mesh=split, in_specs=in_specs, out_specs=out_specs, check_vma=False)
```

```python
import functools

import jax
import jax.numpy as jnp
from jax import lax
from jax.experimental import pallas as pl
from jax.experimental.pallas import tpu as pltpu
from jax.sharding import Mesh
from jax.sharding import PartitionSpec as P

TM = ("tm_0", "tm_hi", "tm_lo")
WAFER = ("wafer_0", "wafer_1")
TM_WAFER = ("tm_0", "tm_hi", "tm_lo", "wafer_0", "wafer_1")


def with_halo(block, sides, width):
    for axis, dim in sides:
        count = lax.axis_size(axis)
        forward = [(i, i + 1) for i in range(count - 1)]
        forward.append((count - 1, 0))
        backward = [(target, source) for source, target in forward]
        low = lax.ppermute(
            lax.slice_in_dim(block, block.shape[dim] - width, None, axis=dim), axis, forward
        )
        high = lax.ppermute(lax.slice_in_dim(block, 0, width, axis=dim), axis, backward)
        block = jnp.concatenate([low, block, high], axis=dim)
    return block


def passed_along(value, axis, by):
    count = lax.axis_size(axis)
    return lax.ppermute(value, axis, [(i, (i + by) % count) for i in range(count)])


def in_blocks(value, dim, count):
    shape = value.shape
    parts = value.reshape(*shape[:dim], count, shape[dim] // count, *shape[dim + 1 :])
    return jnp.moveaxis(parts, dim, 0)


def sum_at_owner(value, axis, dim):
    count = lax.axis_size(axis)
    parts = lax.all_to_all(in_blocks(value, dim, count), axis, 0, 0, tiled=True)
    return jnp.sum(parts, axis=0)


def laid_out(parts, dim):
    shape = list(parts.shape[1:])
    shape[dim] *= parts.shape[0]
    return jnp.moveaxis(parts, 0, dim).reshape(shape)


def copy_for_each(value, axis):
    copies = jnp.broadcast_to(value, (lax.axis_size(axis), *value.shape))
    return lax.all_to_all(copies, axis, split_axis=0, concat_axis=0, tiled=True)


def collect(value, axis, dim):
    return laid_out(copy_for_each(value, axis), dim)


def by_axis(value, axes):
    return functools.reduce(lax.psum, axes, value)


def precondition(gradient, inverse):
    g_i = gradient[:, 0]
    g_q = gradient[:, 1]
    g_u = gradient[:, 2]
    out_i = inverse[:, 0] * g_i + inverse[:, 3] * g_q + inverse[:, 4] * g_u
    out_q = inverse[:, 3] * g_i + inverse[:, 1] * g_q + inverse[:, 5] * g_u
    out_u = inverse[:, 4] * g_i + inverse[:, 5] * g_q + inverse[:, 2] * g_u
    return jnp.stack([out_i, out_q, out_u], axis=1)


SIDE = 128


def split2(value):
    hi = value.astype(jnp.bfloat16)
    lo = (value - hi.astype(jnp.float32)).astype(jnp.bfloat16)
    return hi, lo


def row_onehot(slot, pix, rows):
    row = slot * SIDE + jnp.right_shift(pix, 7)
    ids = lax.broadcasted_iota(jnp.int32, (rows, pix.shape[1]), 0)
    return (ids == row).astype(jnp.bfloat16)


def col_mask(pix):
    col = jnp.bitwise_and(pix, SIDE - 1)
    ids = lax.broadcasted_iota(jnp.int32, (SIDE, pix.shape[1]), 0)
    return ids == col


def stacked_map(mt_ref, lhs_ref):
    hi, lo = split2(mt_ref[...])
    for comp in range(3):
        lhs_ref[comp * SIDE:(comp + 1) * SIDE, :] = hi[comp]
        lhs_ref[(3 + comp) * SIDE:(4 + comp) * SIDE, :] = lo[comp]


def sampled(lhs_ref, at, mask):
    both = jnp.dot(lhs_ref[...], at, preferred_element_type=jnp.float32)
    values = []
    for comp in range(3):
        full = both[comp * SIDE:(comp + 1) * SIDE] + both[(3 + comp) * SIDE:(4 + comp) * SIDE]
        values.append(jnp.sum(jnp.where(mask, full, 0.0), axis=0, keepdims=True))
    return values


def bin_kernel(w_ref, mt_ref, slot_ref, pix_ref, cos_ref, sin_ref, ts_ref, resid_ref, g_ref,
               lhs_ref, rhs_ref, acc_ref):
    stacked_map(mt_ref, lhs_ref)
    acc_ref[...] = jnp.zeros(acc_ref.shape, jnp.float32)
    rows = mt_ref.shape[2]
    nt = (((1,), (1,)), ((), ()))

    def body(d, carry):
        slot = slot_ref[pl.ds(d, 1), :]
        pix = pix_ref[pl.ds(d, 1), :]
        cs = cos_ref[pl.ds(d, 1), :]
        sn = sin_ref[pl.ds(d, 1), :]
        at = row_onehot(slot, pix, rows)
        mask = col_mask(pix)
        v0, v1, v2 = sampled(lhs_ref, at, mask)
        resid = ts_ref[pl.ds(d, 1), :] - (v0 + cs * v1 + sn * v2)
        resid_ref[pl.ds(d, 1), :] = resid
        weighted = w_ref[d] * resid
        for comp, term in ((0, weighted), (1, weighted * cs), (2, weighted * sn)):
            hi, lo = split2(jnp.where(mask, term, 0.0))
            rhs_ref[comp * SIDE:(comp + 1) * SIDE, :] = hi
            rhs_ref[(3 + comp) * SIDE:(4 + comp) * SIDE, :] = lo
        acc_ref[...] += lax.dot_general(at, rhs_ref[...], nt, preferred_element_type=jnp.float32)
        return carry

    lax.fori_loop(0, slot_ref.shape[0], body, 0)
    for s in range(g_ref.shape[0]):
        for comp in range(3):
            rows_s = slice(s * SIDE, (s + 1) * SIDE)
            g_ref[s, comp] = (acc_ref[rows_s, comp * SIDE:(comp + 1) * SIDE]
                              + acc_ref[rows_s, (3 + comp) * SIDE:(4 + comp) * SIDE])


def scan_kernel(mt_ref, slot_ref, pix_ref, cos_ref, sin_ref, out_ref, lhs_ref):
    stacked_map(mt_ref, lhs_ref)
    rows = mt_ref.shape[2]

    def body(d, carry):
        slot = slot_ref[pl.ds(d, 1), :]
        pix = pix_ref[pl.ds(d, 1), :]
        at = row_onehot(slot, pix, rows)
        mask = col_mask(pix)
        v0, v1, v2 = sampled(lhs_ref, at, mask)
        out_ref[pl.ds(d, 1), :] = v0 + cos_ref[pl.ds(d, 1), :] * v1 + sin_ref[pl.ds(d, 1), :] * v2
        return carry

    lax.fori_loop(0, slot_ref.shape[0], body, 0)


def transposed_window(window, local_ids):
    hits = jnp.take(window, local_ids, axis=0)
    count = hits.shape[0]
    grid = hits.reshape(count, 3, SIDE, SIDE)
    return jnp.transpose(grid, (1, 3, 0, 2)).reshape(3, SIDE, count * SIDE)


VMEM = pltpu.MemorySpace.VMEM


def bin_call(weights, mt, slot, pix, cos_two, sin_two, ts):
    dets, samp = slot.shape
    hits = mt.shape[2] // SIDE
    smem = pl.BlockSpec(memory_space=pltpu.SMEM)
    vmem = pl.BlockSpec(memory_space=VMEM)
    return pl.pallas_call(
        bin_kernel,
        out_shape=(
            jax.ShapeDtypeStruct((dets, samp), jnp.float32),
            jax.ShapeDtypeStruct((hits, 3, SIDE, SIDE), jnp.float32),
        ),
        in_specs=[smem] + [vmem] * 6,
        out_specs=(vmem, vmem),
        scratch_shapes=[
            pltpu.VMEM((6 * SIDE, hits * SIDE), jnp.bfloat16),
            pltpu.VMEM((6 * SIDE, samp), jnp.bfloat16),
            pltpu.VMEM((hits * SIDE, 6 * SIDE), jnp.float32),
        ],
    )(weights, mt, slot, pix, cos_two, sin_two, ts)


def scan_call(mt, slot, pix, cos_two, sin_two):
    vmem = pl.BlockSpec(memory_space=VMEM)
    return pl.pallas_call(
        scan_kernel,
        out_shape=jax.ShapeDtypeStruct(slot.shape, jnp.float32),
        in_specs=[vmem] * 5,
        out_specs=vmem,
        scratch_shapes=[pltpu.VMEM((6 * SIDE, mt.shape[2]), jnp.bfloat16)],
    )(mt, slot, pix, cos_two, sin_two)


def local(timestream, noise_weight, hit_slot, tile_pixel, pol_angle, hit_tiles, sky_map, precond):
    tiles_dev = sky_map.shape[0]
    pixels = sky_map.shape[2]
    all_tiles = tiles_dev * lax.axis_size(TM)
    position = lax.axis_index(TM)
    local_ids = jnp.mod(hit_tiles[0] - (position - 1) * tiles_dev, all_tiles)
    doubled = 2.0 * pol_angle[0]
    cos_two = jnp.cos(doubled)
    sin_two = jnp.sin(doubled)
    weights = noise_weight[0]
    slot = hit_slot[0]
    pix = tile_pixel[0]
    wafers = lax.axis_size(WAFER)
    share_width = pixels // wafers
    own_pixels = lax.axis_index(WAFER) * share_width
    precond_share = lax.dynamic_slice_in_dim(precond, own_pixels, share_width, 2)
    precond_window = with_halo(precond_share, ((TM, 0),), tiles_dev)
    window = with_halo(sky_map, ((TM, 0),), tiles_dev)
    mt = transposed_window(window, local_ids)
    resid, binned = bin_call(weights, mt, slot, pix, cos_two, sin_two, timestream[0])
    partial_tiles = binned.reshape(binned.shape[0], 3, pixels)
    near_tiles = jnp.zeros((3 * tiles_dev, 3, pixels), jnp.float32).at[local_ids].add(partial_tiles)
    near_share = sum_at_owner(near_tiles, WAFER, 2)
    lower = near_share[:tiles_dev]
    middle = near_share[tiles_dev : 2 * tiles_dev]
    upper = near_share[2 * tiles_dev :]
    from_below = passed_along(near_share[tiles_dev:], TM, 1)
    from_above = passed_along(near_share[: 2 * tiles_dev], TM, -1)
    from_two_below = passed_along(upper, TM, 2)
    from_two_above = passed_along(lower, TM, -2)
    grad_window = jnp.concatenate(
        [
            lower + from_below[:tiles_dev] + from_two_below,
            middle + from_below[tiles_dev:] + from_above[:tiles_dev],
            upper + from_above[tiles_dev:] + from_two_above,
        ],
        axis=0,
    )
    dir_window_share = precondition(grad_window, precond_window)
    own = slice(tiles_dev, 2 * tiles_dev)
    slope_part = jnp.sum(grad_window[own] * dir_window_share[own])
    dir_window = collect(dir_window_share, WAFER, 2)
    dir_mt = transposed_window(dir_window, local_ids)
    rescanned = scan_call(dir_mt, slot, pix, cos_two, sin_two)
    curve_part = jnp.sum(weights[:, None] * rescanned * rescanned)
    totals = by_axis(jnp.stack([slope_part, curve_part]), ("wafer_1", "wafer_0", "tm_0", "tm_lo", "tm_hi"))
    step_size = totals[0] / totals[1]
    new_map = sky_map + step_size * dir_window[own]
    new_residual = (resid - step_size * rescanned)[None]
    return (new_map, new_residual)


def solution(mesh):
    split = Mesh(mesh.devices.reshape(4, 4, 4, 4, 2), TM_WAFER)
    in_specs = (
        P(TM, WAFER, None),
        P(TM, WAFER),
        P(TM, WAFER, None),
        P(TM, WAFER, None),
        P(TM, WAFER, None),
        P(TM, None),
        P(TM, None, None),
        P(TM, None, None),
    )
    out_specs = (P(TM, None, None), P(TM, WAFER, None))
    return jax.shard_map(local, mesh=split, in_specs=in_specs, out_specs=out_specs, check_vma=False)
```

```python
import functools

import jax
import jax.numpy as jnp
from jax import lax
from jax.experimental import pallas as pl
from jax.experimental.pallas import tpu as pltpu
from jax.sharding import Mesh
from jax.sharding import PartitionSpec as P

TM = ("tm_0", "tm_hi", "tm_lo")
WAFER = ("wafer_0", "wafer_1")
TM_WAFER = ("tm_0", "tm_hi", "tm_lo", "wafer_0", "wafer_1")


def with_halo(block, sides, width):
    for axis, dim in sides:
        count = lax.axis_size(axis)
        forward = [(i, i + 1) for i in range(count - 1)]
        forward.append((count - 1, 0))
        backward = [(target, source) for source, target in forward]
        low = lax.ppermute(
            lax.slice_in_dim(block, block.shape[dim] - width, None, axis=dim), axis, forward
        )
        high = lax.ppermute(lax.slice_in_dim(block, 0, width, axis=dim), axis, backward)
        block = jnp.concatenate([low, block, high], axis=dim)
    return block


def passed_along(value, axis, by):
    count = lax.axis_size(axis)
    return lax.ppermute(value, axis, [(i, (i + by) % count) for i in range(count)])


def in_blocks(value, dim, count):
    shape = value.shape
    parts = value.reshape(*shape[:dim], count, shape[dim] // count, *shape[dim + 1 :])
    return jnp.moveaxis(parts, dim, 0)


def sum_at_owner(value, axis, dim):
    count = lax.axis_size(axis)
    parts = lax.all_to_all(in_blocks(value, dim, count), axis, 0, 0, tiled=True)
    return jnp.sum(parts, axis=0)


def laid_out(parts, dim):
    shape = list(parts.shape[1:])
    shape[dim] *= parts.shape[0]
    return jnp.moveaxis(parts, 0, dim).reshape(shape)


def copy_for_each(value, axis):
    copies = jnp.broadcast_to(value, (lax.axis_size(axis), *value.shape))
    return lax.all_to_all(copies, axis, split_axis=0, concat_axis=0, tiled=True)


def collect(value, axis, dim):
    return laid_out(copy_for_each(value, axis), dim)


def by_axis(value, axes):
    return functools.reduce(lax.psum, axes, value)


def precondition(gradient, inverse):
    g_i = gradient[:, 0]
    g_q = gradient[:, 1]
    g_u = gradient[:, 2]
    out_i = inverse[:, 0] * g_i + inverse[:, 3] * g_q + inverse[:, 4] * g_u
    out_q = inverse[:, 3] * g_i + inverse[:, 1] * g_q + inverse[:, 5] * g_u
    out_u = inverse[:, 4] * g_i + inverse[:, 5] * g_q + inverse[:, 2] * g_u
    return jnp.stack([out_i, out_q, out_u], axis=1)


SIDE = 128


def split2(value):
    hi = value.astype(jnp.bfloat16)
    lo = (value - hi.astype(jnp.float32)).astype(jnp.bfloat16)
    return hi, lo


def row_onehot(slot, pix, rows):
    row = slot * SIDE + jnp.right_shift(pix, 7)
    ids = lax.broadcasted_iota(jnp.int32, (rows, pix.shape[1]), 0)
    return (ids == row).astype(jnp.bfloat16)


def col_mask(pix):
    col = jnp.bitwise_and(pix, SIDE - 1)
    ids = lax.broadcasted_iota(jnp.int32, (SIDE, pix.shape[1]), 0)
    return ids == col


def stacked_map(mt_ref, lhs_ref):
    hi, lo = split2(mt_ref[...])
    for comp in range(3):
        lhs_ref[comp * SIDE:(comp + 1) * SIDE, :] = hi[comp]
        lhs_ref[(3 + comp) * SIDE:(4 + comp) * SIDE, :] = lo[comp]


def sampled(lhs_ref, at, mask):
    both = jnp.dot(lhs_ref[...], at, preferred_element_type=jnp.float32)
    values = []
    for comp in range(3):
        full = both[comp * SIDE:(comp + 1) * SIDE] + both[(3 + comp) * SIDE:(4 + comp) * SIDE]
        values.append(jnp.sum(jnp.where(mask, full, 0.0), axis=0, keepdims=True))
    return values


def bin_kernel(w_ref, mt_ref, slot_ref, pix_ref, cos_ref, sin_ref, ts_ref, resid_ref, g_ref,
               lhs_ref, rhs_ref, acc_ref):
    stacked_map(mt_ref, lhs_ref)
    acc_ref[...] = jnp.zeros(acc_ref.shape, jnp.float32)
    rows = mt_ref.shape[2]
    nt = (((1,), (1,)), ((), ()))

    def body(d, carry):
        slot = slot_ref[pl.ds(d, 1), :]
        pix = pix_ref[pl.ds(d, 1), :]
        cs = cos_ref[pl.ds(d, 1), :]
        sn = sin_ref[pl.ds(d, 1), :]
        at = row_onehot(slot, pix, rows)
        mask = col_mask(pix)
        v0, v1, v2 = sampled(lhs_ref, at, mask)
        resid = ts_ref[pl.ds(d, 1), :] - (v0 + cs * v1 + sn * v2)
        resid_ref[pl.ds(d, 1), :] = resid
        weighted = w_ref[d] * resid
        for comp, term in ((0, weighted), (1, weighted * cs), (2, weighted * sn)):
            hi, lo = split2(jnp.where(mask, term, 0.0))
            rhs_ref[comp * SIDE:(comp + 1) * SIDE, :] = hi
            rhs_ref[(3 + comp) * SIDE:(4 + comp) * SIDE, :] = lo
        acc_ref[...] += lax.dot_general(at, rhs_ref[...], nt, preferred_element_type=jnp.float32)
        return carry

    lax.fori_loop(0, slot_ref.shape[0], body, 0)
    for s in range(g_ref.shape[0]):
        for comp in range(3):
            rows_s = slice(s * SIDE, (s + 1) * SIDE)
            g_ref[s, comp] = (acc_ref[rows_s, comp * SIDE:(comp + 1) * SIDE]
                              + acc_ref[rows_s, (3 + comp) * SIDE:(4 + comp) * SIDE])


def scan_kernel(mt_ref, slot_ref, pix_ref, cos_ref, sin_ref, out_ref, lhs_ref):
    stacked_map(mt_ref, lhs_ref)
    rows = mt_ref.shape[2]

    def body(d, carry):
        slot = slot_ref[pl.ds(d, 1), :]
        pix = pix_ref[pl.ds(d, 1), :]
        at = row_onehot(slot, pix, rows)
        mask = col_mask(pix)
        v0, v1, v2 = sampled(lhs_ref, at, mask)
        out_ref[pl.ds(d, 1), :] = v0 + cos_ref[pl.ds(d, 1), :] * v1 + sin_ref[pl.ds(d, 1), :] * v2
        return carry

    lax.fori_loop(0, slot_ref.shape[0], body, 0)


def transposed_window(window, local_ids):
    hits = jnp.take(window, local_ids, axis=0)
    count = hits.shape[0]
    grid = hits.reshape(count, 3, SIDE, SIDE)
    return jnp.transpose(grid, (1, 3, 0, 2)).reshape(3, SIDE, count * SIDE)


VMEM = pltpu.MemorySpace.VMEM


def bin_call(weights, mt, slot, pix, cos_two, sin_two, ts):
    dets, samp = slot.shape
    hits = mt.shape[2] // SIDE
    smem = pl.BlockSpec(memory_space=pltpu.SMEM)
    vmem = pl.BlockSpec(memory_space=VMEM)
    return pl.pallas_call(
        bin_kernel,
        out_shape=(
            jax.ShapeDtypeStruct((dets, samp), jnp.float32),
            jax.ShapeDtypeStruct((hits, 3, SIDE, SIDE), jnp.float32),
        ),
        in_specs=[smem] + [vmem] * 6,
        out_specs=(vmem, vmem),
        scratch_shapes=[
            pltpu.VMEM((6 * SIDE, hits * SIDE), jnp.bfloat16),
            pltpu.VMEM((6 * SIDE, samp), jnp.bfloat16),
            pltpu.VMEM((hits * SIDE, 6 * SIDE), jnp.float32),
        ],
    )(weights, mt, slot, pix, cos_two, sin_two, ts)


def scan_call(mt, slot, pix, cos_two, sin_two):
    vmem = pl.BlockSpec(memory_space=VMEM)
    return pl.pallas_call(
        scan_kernel,
        out_shape=jax.ShapeDtypeStruct(slot.shape, jnp.float32),
        in_specs=[vmem] * 5,
        out_specs=vmem,
        scratch_shapes=[pltpu.VMEM((6 * SIDE, mt.shape[2]), jnp.bfloat16)],
    )(mt, slot, pix, cos_two, sin_two)


def local(timestream, noise_weight, hit_slot, tile_pixel, pol_angle, hit_tiles, sky_map, precond):
    tiles_dev = sky_map.shape[0]
    pixels = sky_map.shape[2]
    all_tiles = tiles_dev * lax.axis_size(TM)
    position = lax.axis_index(TM)
    local_ids = jnp.mod(hit_tiles[0] - (position - 1) * tiles_dev, all_tiles)
    doubled = 2.0 * pol_angle[0]
    cos_two = jnp.cos(doubled)
    sin_two = jnp.sin(doubled)
    weights = noise_weight[0]
    slot = hit_slot[0]
    pix = tile_pixel[0]
    wafers = lax.axis_size(WAFER)
    share_width = pixels // wafers
    own_pixels = lax.axis_index(WAFER) * share_width
    precond_share = lax.dynamic_slice_in_dim(precond, own_pixels, share_width, 2)
    map_size = 3 * pixels
    both = jnp.concatenate(
        [sky_map.reshape(tiles_dev, map_size), precond_share.reshape(tiles_dev, -1)], axis=1
    )
    both_window = with_halo(both, ((TM, 0),), tiles_dev)
    window = both_window[:, :map_size].reshape(3 * tiles_dev, 3, pixels)
    precond_window = both_window[:, map_size:].reshape(3 * tiles_dev, 6, share_width)
    mt = transposed_window(window, local_ids)
    resid, binned = bin_call(weights, mt, slot, pix, cos_two, sin_two, timestream[0])
    partial_tiles = binned.reshape(binned.shape[0], 3, pixels)
    near_tiles = jnp.zeros((3 * tiles_dev, 3, pixels), jnp.float32).at[local_ids].add(partial_tiles)
    near_share = sum_at_owner(near_tiles, WAFER, 2)
    lower = near_share[:tiles_dev]
    middle = near_share[tiles_dev : 2 * tiles_dev]
    upper = near_share[2 * tiles_dev :]
    from_below = passed_along(near_share[tiles_dev:], TM, 1)
    from_above = passed_along(near_share[: 2 * tiles_dev], TM, -1)
    from_two_below = passed_along(upper, TM, 2)
    from_two_above = passed_along(lower, TM, -2)
    grad_window = jnp.concatenate(
        [
            lower + from_below[:tiles_dev] + from_two_below,
            middle + from_below[tiles_dev:] + from_above[:tiles_dev],
            upper + from_above[tiles_dev:] + from_two_above,
        ],
        axis=0,
    )
    dir_window_share = precondition(grad_window, precond_window)
    own = slice(tiles_dev, 2 * tiles_dev)
    slope_part = jnp.sum(grad_window[own] * dir_window_share[own])
    dir_window = collect(dir_window_share, WAFER, 2)
    dir_mt = transposed_window(dir_window, local_ids)
    rescanned = scan_call(dir_mt, slot, pix, cos_two, sin_two)
    curve_part = jnp.sum(weights[:, None] * rescanned * rescanned)
    totals = by_axis(jnp.stack([slope_part, curve_part]), ("wafer_1", "wafer_0", "tm_0", "tm_lo", "tm_hi"))
    step_size = totals[0] / totals[1]
    new_map = sky_map + step_size * dir_window[own]
    new_residual = (resid - step_size * rescanned)[None]
    return (new_map, new_residual)


def solution(mesh):
    split = Mesh(mesh.devices.reshape(4, 4, 4, 4, 2), TM_WAFER)
    in_specs = (
        P(TM, WAFER, None),
        P(TM, WAFER),
        P(TM, WAFER, None),
        P(TM, WAFER, None),
        P(TM, WAFER, None),
        P(TM, None),
        P(TM, None, None),
        P(TM, None, None),
    )
    out_specs = (P(TM, None, None), P(TM, WAFER, None))
    return jax.shard_map(local, mesh=split, in_specs=in_specs, out_specs=out_specs, check_vma=False)
```

```python
import functools

import jax
import jax.numpy as jnp
from jax import lax
from jax.experimental import pallas as pl
from jax.experimental.pallas import tpu as pltpu
from jax.sharding import Mesh
from jax.sharding import PartitionSpec as P

TM = ("tm_0", "tm_hi", "tm_lo")
WAFER = ("wafer_0", "wafer_1")
TM_WAFER = ("tm_0", "tm_hi", "tm_lo", "wafer_0", "wafer_1")


def with_halo(block, sides, width):
    for axis, dim in sides:
        count = lax.axis_size(axis)
        forward = [(i, i + 1) for i in range(count - 1)]
        forward.append((count - 1, 0))
        backward = [(target, source) for source, target in forward]
        low = lax.ppermute(
            lax.slice_in_dim(block, block.shape[dim] - width, None, axis=dim), axis, forward
        )
        high = lax.ppermute(lax.slice_in_dim(block, 0, width, axis=dim), axis, backward)
        block = jnp.concatenate([low, block, high], axis=dim)
    return block


def passed_along(value, axis, by):
    count = lax.axis_size(axis)
    return lax.ppermute(value, axis, [(i, (i + by) % count) for i in range(count)])


def in_blocks(value, dim, count):
    shape = value.shape
    parts = value.reshape(*shape[:dim], count, shape[dim] // count, *shape[dim + 1 :])
    return jnp.moveaxis(parts, dim, 0)


def sum_at_owner(value, axis, dim):
    count = lax.axis_size(axis)
    parts = lax.all_to_all(in_blocks(value, dim, count), axis, 0, 0, tiled=True)
    return jnp.sum(parts, axis=0)


def laid_out(parts, dim):
    shape = list(parts.shape[1:])
    shape[dim] *= parts.shape[0]
    return jnp.moveaxis(parts, 0, dim).reshape(shape)


def copy_for_each(value, axis):
    copies = jnp.broadcast_to(value, (lax.axis_size(axis), *value.shape))
    return lax.all_to_all(copies, axis, split_axis=0, concat_axis=0, tiled=True)


def collect(value, axis, dim):
    return laid_out(copy_for_each(value, axis), dim)


def by_axis(value, axes):
    return functools.reduce(lax.psum, axes, value)


def precondition(gradient, inverse):
    g_i = gradient[:, 0]
    g_q = gradient[:, 1]
    g_u = gradient[:, 2]
    out_i = inverse[:, 0] * g_i + inverse[:, 3] * g_q + inverse[:, 4] * g_u
    out_q = inverse[:, 3] * g_i + inverse[:, 1] * g_q + inverse[:, 5] * g_u
    out_u = inverse[:, 4] * g_i + inverse[:, 5] * g_q + inverse[:, 2] * g_u
    return jnp.stack([out_i, out_q, out_u], axis=1)


SIDE = 128


def split2(value):
    hi = value.astype(jnp.bfloat16)
    lo = (value - hi.astype(jnp.float32)).astype(jnp.bfloat16)
    return hi, lo


def row_onehot(slot, pix, rows):
    row = slot * SIDE + jnp.right_shift(pix, 7)
    ids = lax.broadcasted_iota(jnp.int32, (rows, pix.shape[1]), 0)
    return (ids == row).astype(jnp.bfloat16)


def col_mask(pix):
    col = jnp.bitwise_and(pix, SIDE - 1)
    ids = lax.broadcasted_iota(jnp.int32, (SIDE, pix.shape[1]), 0)
    return ids == col


def stacked_map(ids_ref, win_ref, lhs_ref):
    for s in range(ids_ref.shape[0]):
        tile_id = ids_ref[s]
        for comp in range(3):
            hi, lo = split2(win_ref[tile_id, comp].T)
            cols = slice(s * SIDE, (s + 1) * SIDE)
            lhs_ref[comp * SIDE:(comp + 1) * SIDE, cols] = hi
            lhs_ref[(3 + comp) * SIDE:(4 + comp) * SIDE, cols] = lo


def sampled(lhs_ref, at, mask):
    both = jnp.dot(lhs_ref[...], at, preferred_element_type=jnp.float32)
    values = []
    for comp in range(3):
        full = both[comp * SIDE:(comp + 1) * SIDE] + both[(3 + comp) * SIDE:(4 + comp) * SIDE]
        values.append(jnp.sum(jnp.where(mask, full, 0.0), axis=0, keepdims=True))
    return values


def bin_kernel(ids_ref, w_ref, win_ref, slot_ref, pix_ref, cos_ref, sin_ref, ts_ref, resid_ref, g_ref,
               lhs_ref, rhs_ref, acc_ref):
    stacked_map(ids_ref, win_ref, lhs_ref)
    acc_ref[...] = jnp.zeros(acc_ref.shape, jnp.float32)
    rows = lhs_ref.shape[1]
    nt = (((1,), (1,)), ((), ()))

    def body(d, carry):
        slot = slot_ref[pl.ds(d, 1), :]
        pix = pix_ref[pl.ds(d, 1), :]
        cs = cos_ref[pl.ds(d, 1), :]
        sn = sin_ref[pl.ds(d, 1), :]
        at = row_onehot(slot, pix, rows)
        mask = col_mask(pix)
        v0, v1, v2 = sampled(lhs_ref, at, mask)
        resid = ts_ref[pl.ds(d, 1), :] - (v0 + cs * v1 + sn * v2)
        resid_ref[pl.ds(d, 1), :] = resid
        weighted = w_ref[d] * resid
        for comp, term in ((0, weighted), (1, weighted * cs), (2, weighted * sn)):
            hi, lo = split2(jnp.where(mask, term, 0.0))
            rhs_ref[comp * SIDE:(comp + 1) * SIDE, :] = hi
            rhs_ref[(3 + comp) * SIDE:(4 + comp) * SIDE, :] = lo
        acc_ref[...] += lax.dot_general(at, rhs_ref[...], nt, preferred_element_type=jnp.float32)
        return carry

    lax.fori_loop(0, slot_ref.shape[0], body, 0)
    g_ref[...] = jnp.zeros(g_ref.shape, jnp.float32)
    for s in range(ids_ref.shape[0]):
        for comp in range(3):
            rows_s = slice(s * SIDE, (s + 1) * SIDE)
            g_ref[ids_ref[s], comp] = (acc_ref[rows_s, comp * SIDE:(comp + 1) * SIDE]
                              + acc_ref[rows_s, (3 + comp) * SIDE:(4 + comp) * SIDE])


def scan_kernel(ids_ref, win_ref, slot_ref, pix_ref, cos_ref, sin_ref, out_ref, lhs_ref):
    stacked_map(ids_ref, win_ref, lhs_ref)
    rows = lhs_ref.shape[1]

    def body(d, carry):
        slot = slot_ref[pl.ds(d, 1), :]
        pix = pix_ref[pl.ds(d, 1), :]
        at = row_onehot(slot, pix, rows)
        mask = col_mask(pix)
        v0, v1, v2 = sampled(lhs_ref, at, mask)
        out_ref[pl.ds(d, 1), :] = v0 + cos_ref[pl.ds(d, 1), :] * v1 + sin_ref[pl.ds(d, 1), :] * v2
        return carry

    lax.fori_loop(0, slot_ref.shape[0], body, 0)


VMEM = pltpu.MemorySpace.VMEM


def bin_call(local_ids, weights, win, slot, pix, cos_two, sin_two, ts):
    dets, samp = slot.shape
    hits = local_ids.shape[0]
    smem = pl.BlockSpec(memory_space=pltpu.SMEM)
    vmem = pl.BlockSpec(memory_space=VMEM)
    return pl.pallas_call(
        bin_kernel,
        out_shape=(
            jax.ShapeDtypeStruct((dets, samp), jnp.float32),
            jax.ShapeDtypeStruct(win.shape, jnp.float32),
        ),
        in_specs=[smem, smem] + [vmem] * 6,
        out_specs=(vmem, vmem),
        scratch_shapes=[
            pltpu.VMEM((6 * SIDE, hits * SIDE), jnp.bfloat16),
            pltpu.VMEM((6 * SIDE, samp), jnp.bfloat16),
            pltpu.VMEM((hits * SIDE, 6 * SIDE), jnp.float32),
        ],
    )(local_ids, weights, win, slot, pix, cos_two, sin_two, ts)


def scan_call(local_ids, win, slot, pix, cos_two, sin_two):
    hits = local_ids.shape[0]
    smem = pl.BlockSpec(memory_space=pltpu.SMEM)
    vmem = pl.BlockSpec(memory_space=VMEM)
    return pl.pallas_call(
        scan_kernel,
        out_shape=jax.ShapeDtypeStruct(slot.shape, jnp.float32),
        in_specs=[smem] + [vmem] * 5,
        out_specs=vmem,
        scratch_shapes=[pltpu.VMEM((6 * SIDE, hits * SIDE), jnp.bfloat16)],
    )(local_ids, win, slot, pix, cos_two, sin_two)


def as_grid(tiles):
    return tiles.reshape(tiles.shape[0], 3, SIDE, SIDE)


def local(timestream, noise_weight, hit_slot, tile_pixel, pol_angle, hit_tiles, sky_map, precond):
    tiles_dev = sky_map.shape[0]
    pixels = sky_map.shape[2]
    all_tiles = tiles_dev * lax.axis_size(TM)
    position = lax.axis_index(TM)
    local_ids = jnp.mod(hit_tiles[0] - (position - 1) * tiles_dev, all_tiles)
    doubled = 2.0 * pol_angle[0]
    cos_two = jnp.cos(doubled)
    sin_two = jnp.sin(doubled)
    weights = noise_weight[0]
    slot = hit_slot[0]
    pix = tile_pixel[0]
    window = with_halo(as_grid(sky_map), ((TM, 0),), tiles_dev)
    resid, binned = bin_call(local_ids, weights, window, slot, pix, cos_two, sin_two, timestream[0])
    near_tiles = binned.reshape(binned.shape[0], 3, pixels)
    from_upper = passed_along(near_tiles[:tiles_dev], TM, -1)
    from_lower = passed_along(near_tiles[2 * tiles_dev :], TM, 1)
    owned_tiles = near_tiles[tiles_dev : 2 * tiles_dev] + from_upper + from_lower
    grad_share = sum_at_owner(owned_tiles, WAFER, 2)
    share_width = grad_share.shape[2]
    inverse_share = lax.dynamic_slice_in_dim(
        precond, lax.axis_index(WAFER) * share_width, share_width, 2
    )
    dir_share = precondition(grad_share, inverse_share)
    slope_part = jnp.sum(grad_share * dir_share)
    direction = collect(dir_share, WAFER, 2)
    dir_window = with_halo(as_grid(direction), ((TM, 0),), tiles_dev)
    rescanned = scan_call(local_ids, dir_window, slot, pix, cos_two, sin_two)
    curve_part = jnp.sum(weights[:, None] * rescanned * rescanned)
    totals = by_axis(jnp.stack([slope_part, curve_part]), ("wafer_1", "wafer_0", "tm_0", "tm_lo", "tm_hi"))
    step_size = totals[0] / totals[1]
    new_map = sky_map + step_size * direction
    new_residual = (resid - step_size * rescanned)[None]
    return (new_map, new_residual)


def solution(mesh):
    split = Mesh(mesh.devices.reshape(4, 4, 4, 4, 2), TM_WAFER)
    in_specs = (
        P(TM, WAFER, None),
        P(TM, WAFER),
        P(TM, WAFER, None),
        P(TM, WAFER, None),
        P(TM, WAFER, None),
        P(TM, None),
        P(TM, None, None),
        P(TM, None, None),
    )
    out_specs = (P(TM, None, None), P(TM, WAFER, None))
    return jax.shard_map(local, mesh=split, in_specs=in_specs, out_specs=out_specs, check_vma=False)
```

```python
import functools

import jax
import jax.numpy as jnp
from jax import lax
from jax.experimental import pallas as pl
from jax.experimental.pallas import tpu as pltpu
from jax.sharding import Mesh
from jax.sharding import PartitionSpec as P

TM = ("tm_0", "tm_hi", "tm_lo")
WAFER = ("wafer_0", "wafer_1")
TM_WAFER = ("tm_0", "tm_hi", "tm_lo", "wafer_0", "wafer_1")


def with_halo(block, sides, width):
    for axis, dim in sides:
        count = lax.axis_size(axis)
        forward = [(i, i + 1) for i in range(count - 1)]
        forward.append((count - 1, 0))
        backward = [(target, source) for source, target in forward]
        low = lax.ppermute(
            lax.slice_in_dim(block, block.shape[dim] - width, None, axis=dim), axis, forward
        )
        high = lax.ppermute(lax.slice_in_dim(block, 0, width, axis=dim), axis, backward)
        block = jnp.concatenate([low, block, high], axis=dim)
    return block


def passed_along(value, axis, by):
    count = lax.axis_size(axis)
    return lax.ppermute(value, axis, [(i, (i + by) % count) for i in range(count)])


def in_blocks(value, dim, count):
    shape = value.shape
    parts = value.reshape(*shape[:dim], count, shape[dim] // count, *shape[dim + 1 :])
    return jnp.moveaxis(parts, dim, 0)


def sum_at_owner(value, axis, dim):
    count = lax.axis_size(axis)
    parts = lax.all_to_all(in_blocks(value, dim, count), axis, 0, 0, tiled=True)
    return jnp.sum(parts, axis=0)


def laid_out(parts, dim):
    shape = list(parts.shape[1:])
    shape[dim] *= parts.shape[0]
    return jnp.moveaxis(parts, 0, dim).reshape(shape)


def copy_for_each(value, axis):
    copies = jnp.broadcast_to(value, (lax.axis_size(axis), *value.shape))
    return lax.all_to_all(copies, axis, split_axis=0, concat_axis=0, tiled=True)


def collect(value, axis, dim):
    return laid_out(copy_for_each(value, axis), dim)


def by_axis(value, axes):
    return functools.reduce(lax.psum, axes, value)


def precondition(gradient, inverse):
    g_i = gradient[:, 0]
    g_q = gradient[:, 1]
    g_u = gradient[:, 2]
    out_i = inverse[:, 0] * g_i + inverse[:, 3] * g_q + inverse[:, 4] * g_u
    out_q = inverse[:, 3] * g_i + inverse[:, 1] * g_q + inverse[:, 5] * g_u
    out_u = inverse[:, 4] * g_i + inverse[:, 5] * g_q + inverse[:, 2] * g_u
    return jnp.stack([out_i, out_q, out_u], axis=1)


SIDE = 128


def split2(value):
    hi = value.astype(jnp.bfloat16)
    lo = (value - hi.astype(jnp.float32)).astype(jnp.bfloat16)
    return hi, lo


def row_onehot(slot, pix, rows):
    row = slot * SIDE + jnp.right_shift(pix, 7)
    ids = lax.broadcasted_iota(jnp.int32, (rows, pix.shape[1]), 0)
    return (ids == row).astype(jnp.bfloat16)


def col_mask(pix):
    col = jnp.bitwise_and(pix, SIDE - 1)
    ids = lax.broadcasted_iota(jnp.int32, (SIDE, pix.shape[1]), 0)
    return ids == col


def stacked_map(ids_ref, win_ref, lhs_ref):
    for s in range(ids_ref.shape[0]):
        tile_id = ids_ref[s]
        for comp in range(3):
            hi, lo = split2(win_ref[tile_id, comp].T)
            cols = slice(s * SIDE, (s + 1) * SIDE)
            lhs_ref[comp * SIDE:(comp + 1) * SIDE, cols] = hi
            lhs_ref[(3 + comp) * SIDE:(4 + comp) * SIDE, cols] = lo


def sampled(lhs_ref, at, mask):
    both = jnp.dot(lhs_ref[...], at, preferred_element_type=jnp.float32)
    values = []
    for comp in range(3):
        full = both[comp * SIDE:(comp + 1) * SIDE] + both[(3 + comp) * SIDE:(4 + comp) * SIDE]
        values.append(jnp.sum(jnp.where(mask, full, 0.0), axis=0, keepdims=True))
    return values


def bin_kernel(ids_ref, w_ref, win_ref, slot_ref, pix_ref, cos_ref, sin_ref, ts_ref, resid_ref, g_ref,
               lhs_ref, rhs_ref, acc_ref):
    stacked_map(ids_ref, win_ref, lhs_ref)
    acc_ref[...] = jnp.zeros(acc_ref.shape, jnp.float32)
    rows = lhs_ref.shape[1]
    nt = (((1,), (1,)), ((), ()))

    def body(d, carry):
        slot = slot_ref[pl.ds(d, 1), :]
        pix = pix_ref[pl.ds(d, 1), :]
        cs = cos_ref[pl.ds(d, 1), :]
        sn = sin_ref[pl.ds(d, 1), :]
        at = row_onehot(slot, pix, rows)
        mask = col_mask(pix)
        v0, v1, v2 = sampled(lhs_ref, at, mask)
        resid = ts_ref[pl.ds(d, 1), :] - (v0 + cs * v1 + sn * v2)
        resid_ref[pl.ds(d, 1), :] = resid
        weighted = w_ref[d] * resid
        for comp, term in ((0, weighted), (1, weighted * cs), (2, weighted * sn)):
            hi, lo = split2(jnp.where(mask, term, 0.0))
            rhs_ref[comp * SIDE:(comp + 1) * SIDE, :] = hi
            rhs_ref[(3 + comp) * SIDE:(4 + comp) * SIDE, :] = lo
        acc_ref[...] += lax.dot_general(at, rhs_ref[...], nt, preferred_element_type=jnp.float32)
        return carry

    lax.fori_loop(0, slot_ref.shape[0], body, 0)
    g_ref[...] = jnp.zeros(g_ref.shape, jnp.float32)
    for s in range(ids_ref.shape[0]):
        for comp in range(3):
            rows_s = slice(s * SIDE, (s + 1) * SIDE)
            g_ref[ids_ref[s], comp] = (acc_ref[rows_s, comp * SIDE:(comp + 1) * SIDE]
                              + acc_ref[rows_s, (3 + comp) * SIDE:(4 + comp) * SIDE])


def scan_kernel(ids_ref, w_ref, slope_ref, win_ref, slot_ref, pix_ref, cos_ref, sin_ref, out_ref,
                totals_ref, lhs_ref):
    stacked_map(ids_ref, win_ref, lhs_ref)
    rows = lhs_ref.shape[1]

    def body(d, curve):
        slot = slot_ref[pl.ds(d, 1), :]
        pix = pix_ref[pl.ds(d, 1), :]
        at = row_onehot(slot, pix, rows)
        mask = col_mask(pix)
        v0, v1, v2 = sampled(lhs_ref, at, mask)
        value = v0 + cos_ref[pl.ds(d, 1), :] * v1 + sin_ref[pl.ds(d, 1), :] * v2
        out_ref[pl.ds(d, 1), :] = value
        return curve + w_ref[d] * value * value

    curve = lax.fori_loop(0, slot_ref.shape[0], body, jnp.zeros(cos_ref.shape[1:], jnp.float32)[None])
    curve_sum = jnp.sum(curve, axis=1, keepdims=True)
    lane = lax.broadcasted_iota(jnp.int32, totals_ref.shape, 1)
    totals_ref[...] = jnp.where(lane == 0, slope_ref[0], jnp.where(lane == 1, curve_sum, 0.0))


VMEM = pltpu.MemorySpace.VMEM


def bin_call(local_ids, weights, win, slot, pix, cos_two, sin_two, ts):
    dets, samp = slot.shape
    hits = local_ids.shape[0]
    smem = pl.BlockSpec(memory_space=pltpu.SMEM)
    vmem = pl.BlockSpec(memory_space=VMEM)
    return pl.pallas_call(
        bin_kernel,
        out_shape=(
            jax.ShapeDtypeStruct((dets, samp), jnp.float32),
            jax.ShapeDtypeStruct(win.shape, jnp.float32),
        ),
        in_specs=[smem, smem] + [vmem] * 6,
        out_specs=(vmem, vmem),
        scratch_shapes=[
            pltpu.VMEM((6 * SIDE, hits * SIDE), jnp.bfloat16),
            pltpu.VMEM((6 * SIDE, samp), jnp.bfloat16),
            pltpu.VMEM((hits * SIDE, 6 * SIDE), jnp.float32),
        ],
    )(local_ids, weights, win, slot, pix, cos_two, sin_two, ts)


def scan_call(local_ids, weights, slope, win, slot, pix, cos_two, sin_two):
    hits = local_ids.shape[0]
    smem = pl.BlockSpec(memory_space=pltpu.SMEM)
    vmem = pl.BlockSpec(memory_space=VMEM)
    return pl.pallas_call(
        scan_kernel,
        out_shape=(
            jax.ShapeDtypeStruct(slot.shape, jnp.float32),
            jax.ShapeDtypeStruct((1, SIDE), jnp.float32),
        ),
        in_specs=[smem] * 3 + [vmem] * 5,
        out_specs=(vmem, vmem),
        scratch_shapes=[pltpu.VMEM((6 * SIDE, hits * SIDE), jnp.bfloat16)],
    )(local_ids, weights, slope, win, slot, pix, cos_two, sin_two)


def as_grid(tiles):
    return tiles.reshape(tiles.shape[0], 3, SIDE, SIDE)


def local(timestream, noise_weight, hit_slot, tile_pixel, pol_angle, hit_tiles, sky_map, precond):
    tiles_dev = sky_map.shape[0]
    pixels = sky_map.shape[2]
    all_tiles = tiles_dev * lax.axis_size(TM)
    position = lax.axis_index(TM)
    local_ids = jnp.mod(hit_tiles[0] - (position - 1) * tiles_dev, all_tiles)
    doubled = 2.0 * pol_angle[0]
    cos_two = jnp.cos(doubled)
    sin_two = jnp.sin(doubled)
    weights = noise_weight[0]
    slot = hit_slot[0]
    pix = tile_pixel[0]
    window = with_halo(as_grid(sky_map), ((TM, 0),), tiles_dev)
    resid, binned = bin_call(local_ids, weights, window, slot, pix, cos_two, sin_two, timestream[0])
    near_tiles = binned.reshape(binned.shape[0], 3, pixels)
    from_upper = passed_along(near_tiles[:tiles_dev], TM, -1)
    from_lower = passed_along(near_tiles[2 * tiles_dev :], TM, 1)
    owned_tiles = near_tiles[tiles_dev : 2 * tiles_dev] + from_upper + from_lower
    grad_share = sum_at_owner(owned_tiles, WAFER, 2)
    share_width = grad_share.shape[2]
    inverse_share = lax.dynamic_slice_in_dim(
        precond, lax.axis_index(WAFER) * share_width, share_width, 2
    )
    dir_share = precondition(grad_share, inverse_share)
    slope_part = jnp.sum(grad_share * dir_share)
    direction = collect(dir_share, WAFER, 2)
    dir_window = with_halo(as_grid(direction), ((TM, 0),), tiles_dev)
    rescanned, parts = scan_call(
        local_ids, weights, slope_part.reshape(1), dir_window, slot, pix, cos_two, sin_two
    )
    totals = by_axis(parts, ("wafer_1", "wafer_0", "tm_0", "tm_lo", "tm_hi"))
    step_size = totals[0, 0] / totals[0, 1]
    new_map = sky_map + step_size * direction
    new_residual = (resid - step_size * rescanned)[None]
    return (new_map, new_residual)


def solution(mesh):
    split = Mesh(mesh.devices.reshape(4, 4, 4, 4, 2), TM_WAFER)
    in_specs = (
        P(TM, WAFER, None),
        P(TM, WAFER),
        P(TM, WAFER, None),
        P(TM, WAFER, None),
        P(TM, WAFER, None),
        P(TM, None),
        P(TM, None, None),
        P(TM, None, None),
    )
    out_specs = (P(TM, None, None), P(TM, WAFER, None))
    return jax.shard_map(local, mesh=split, in_specs=in_specs, out_specs=out_specs, check_vma=False)
```

```python
import functools

import jax
import jax.numpy as jnp
from jax import lax
from jax.experimental import pallas as pl
from jax.experimental.pallas import tpu as pltpu
from jax.sharding import Mesh
from jax.sharding import PartitionSpec as P

TM = ("tm_0", "tm_hi", "tm_lo")
WAFER = ("wafer_0", "wafer_1")
TM_WAFER = ("tm_0", "tm_hi", "tm_lo", "wafer_0", "wafer_1")


def with_halo(block, sides, width):
    for axis, dim in sides:
        count = lax.axis_size(axis)
        forward = [(i, i + 1) for i in range(count - 1)]
        forward.append((count - 1, 0))
        backward = [(target, source) for source, target in forward]
        low = lax.ppermute(
            lax.slice_in_dim(block, block.shape[dim] - width, None, axis=dim), axis, forward
        )
        high = lax.ppermute(lax.slice_in_dim(block, 0, width, axis=dim), axis, backward)
        block = jnp.concatenate([low, block, high], axis=dim)
    return block


def passed_along(value, axis, by):
    count = lax.axis_size(axis)
    return lax.ppermute(value, axis, [(i, (i + by) % count) for i in range(count)])


def in_blocks(value, dim, count):
    shape = value.shape
    parts = value.reshape(*shape[:dim], count, shape[dim] // count, *shape[dim + 1 :])
    return jnp.moveaxis(parts, dim, 0)


def sum_at_owner(value, axis, dim):
    count = lax.axis_size(axis)
    parts = lax.all_to_all(in_blocks(value, dim, count), axis, 0, 0, tiled=True)
    return jnp.sum(parts, axis=0)


def laid_out(parts, dim):
    shape = list(parts.shape[1:])
    shape[dim] *= parts.shape[0]
    return jnp.moveaxis(parts, 0, dim).reshape(shape)


def copy_for_each(value, axis):
    copies = jnp.broadcast_to(value, (lax.axis_size(axis), *value.shape))
    return lax.all_to_all(copies, axis, split_axis=0, concat_axis=0, tiled=True)


def collect(value, axis, dim):
    return laid_out(copy_for_each(value, axis), dim)


def summed_by_exchange(value, axis):
    return jnp.sum(copy_for_each(value, axis), axis=0)


def by_axis(value, axes):
    return functools.reduce(lax.psum, axes, value)


def precondition(gradient, inverse):
    g_i = gradient[:, 0]
    g_q = gradient[:, 1]
    g_u = gradient[:, 2]
    out_i = inverse[:, 0] * g_i + inverse[:, 3] * g_q + inverse[:, 4] * g_u
    out_q = inverse[:, 3] * g_i + inverse[:, 1] * g_q + inverse[:, 5] * g_u
    out_u = inverse[:, 4] * g_i + inverse[:, 5] * g_q + inverse[:, 2] * g_u
    return jnp.stack([out_i, out_q, out_u], axis=1)


SIDE = 128


def split2(value):
    hi = value.astype(jnp.bfloat16)
    lo = (value - hi.astype(jnp.float32)).astype(jnp.bfloat16)
    return hi, lo


def row_onehot(slot, pix, rows):
    row = slot * SIDE + jnp.right_shift(pix, 7)
    ids = lax.broadcasted_iota(jnp.int32, (rows, pix.shape[1]), 0)
    return (ids == row).astype(jnp.bfloat16)


def col_mask(pix):
    col = jnp.bitwise_and(pix, SIDE - 1)
    ids = lax.broadcasted_iota(jnp.int32, (SIDE, pix.shape[1]), 0)
    return ids == col


def stacked_map(ids_ref, win_ref, lhs_ref):
    for s in range(ids_ref.shape[0]):
        tile_id = ids_ref[s]
        for comp in range(3):
            hi, lo = split2(win_ref[tile_id, comp].T)
            cols = slice(s * SIDE, (s + 1) * SIDE)
            lhs_ref[comp * SIDE:(comp + 1) * SIDE, cols] = hi
            lhs_ref[(3 + comp) * SIDE:(4 + comp) * SIDE, cols] = lo


def sampled(lhs_ref, at, mask):
    both = jnp.dot(lhs_ref[...], at, preferred_element_type=jnp.float32)
    values = []
    for comp in range(3):
        full = both[comp * SIDE:(comp + 1) * SIDE] + both[(3 + comp) * SIDE:(4 + comp) * SIDE]
        values.append(jnp.sum(jnp.where(mask, full, 0.0), axis=0, keepdims=True))
    return values


def bin_kernel(ids_ref, w_ref, win_ref, slot_ref, pix_ref, cos_ref, sin_ref, ts_ref, resid_ref, g_ref,
               lhs_ref, rhs_ref, acc_ref):
    stacked_map(ids_ref, win_ref, lhs_ref)
    acc_ref[...] = jnp.zeros(acc_ref.shape, jnp.float32)
    rows = lhs_ref.shape[1]
    nt = (((1,), (1,)), ((), ()))

    def body(d, carry):
        slot = slot_ref[pl.ds(d, 1), :]
        pix = pix_ref[pl.ds(d, 1), :]
        cs = cos_ref[pl.ds(d, 1), :]
        sn = sin_ref[pl.ds(d, 1), :]
        at = row_onehot(slot, pix, rows)
        mask = col_mask(pix)
        v0, v1, v2 = sampled(lhs_ref, at, mask)
        resid = ts_ref[pl.ds(d, 1), :] - (v0 + cs * v1 + sn * v2)
        resid_ref[pl.ds(d, 1), :] = resid
        weighted = w_ref[d] * resid
        for comp, term in ((0, weighted), (1, weighted * cs), (2, weighted * sn)):
            hi, lo = split2(jnp.where(mask, term, 0.0))
            rhs_ref[comp * SIDE:(comp + 1) * SIDE, :] = hi
            rhs_ref[(3 + comp) * SIDE:(4 + comp) * SIDE, :] = lo
        acc_ref[...] += lax.dot_general(at, rhs_ref[...], nt, preferred_element_type=jnp.float32)
        return carry

    lax.fori_loop(0, slot_ref.shape[0], body, 0)
    g_ref[...] = jnp.zeros(g_ref.shape, jnp.float32)
    for s in range(ids_ref.shape[0]):
        for comp in range(3):
            rows_s = slice(s * SIDE, (s + 1) * SIDE)
            g_ref[ids_ref[s], comp] = (acc_ref[rows_s, comp * SIDE:(comp + 1) * SIDE]
                              + acc_ref[rows_s, (3 + comp) * SIDE:(4 + comp) * SIDE])


def scan_kernel(ids_ref, w_ref, slope_ref, win_ref, slot_ref, pix_ref, cos_ref, sin_ref, out_ref,
                totals_ref, lhs_ref):
    stacked_map(ids_ref, win_ref, lhs_ref)
    rows = lhs_ref.shape[1]

    def body(d, curve):
        slot = slot_ref[pl.ds(d, 1), :]
        pix = pix_ref[pl.ds(d, 1), :]
        at = row_onehot(slot, pix, rows)
        mask = col_mask(pix)
        v0, v1, v2 = sampled(lhs_ref, at, mask)
        value = v0 + cos_ref[pl.ds(d, 1), :] * v1 + sin_ref[pl.ds(d, 1), :] * v2
        out_ref[pl.ds(d, 1), :] = value
        return curve + w_ref[d] * value * value

    curve = lax.fori_loop(0, slot_ref.shape[0], body, jnp.zeros(cos_ref.shape[1:], jnp.float32)[None])
    curve_sum = jnp.sum(curve, axis=1, keepdims=True)
    lane = lax.broadcasted_iota(jnp.int32, totals_ref.shape, 1)
    totals_ref[...] = jnp.where(lane == 0, slope_ref[0], jnp.where(lane == 1, curve_sum, 0.0))


VMEM = pltpu.MemorySpace.VMEM


def bin_call(local_ids, weights, win, slot, pix, cos_two, sin_two, ts):
    dets, samp = slot.shape
    hits = local_ids.shape[0]
    smem = pl.BlockSpec(memory_space=pltpu.SMEM)
    vmem = pl.BlockSpec(memory_space=VMEM)
    return pl.pallas_call(
        bin_kernel,
        out_shape=(
            jax.ShapeDtypeStruct((dets, samp), jnp.float32),
            jax.ShapeDtypeStruct(win.shape, jnp.float32),
        ),
        in_specs=[smem, smem] + [vmem] * 6,
        out_specs=(vmem, vmem),
        scratch_shapes=[
            pltpu.VMEM((6 * SIDE, hits * SIDE), jnp.bfloat16),
            pltpu.VMEM((6 * SIDE, samp), jnp.bfloat16),
            pltpu.VMEM((hits * SIDE, 6 * SIDE), jnp.float32),
        ],
    )(local_ids, weights, win, slot, pix, cos_two, sin_two, ts)


def scan_call(local_ids, weights, slope, win, slot, pix, cos_two, sin_two):
    hits = local_ids.shape[0]
    smem = pl.BlockSpec(memory_space=pltpu.SMEM)
    vmem = pl.BlockSpec(memory_space=VMEM)
    return pl.pallas_call(
        scan_kernel,
        out_shape=(
            jax.ShapeDtypeStruct(slot.shape, jnp.float32),
            jax.ShapeDtypeStruct((1, SIDE), jnp.float32),
        ),
        in_specs=[smem] * 3 + [vmem] * 5,
        out_specs=(vmem, vmem),
        scratch_shapes=[pltpu.VMEM((6 * SIDE, hits * SIDE), jnp.bfloat16)],
    )(local_ids, weights, slope, win, slot, pix, cos_two, sin_two)


def as_grid(tiles):
    return tiles.reshape(tiles.shape[0], 3, SIDE, SIDE)


def local(timestream, noise_weight, hit_slot, tile_pixel, pol_angle, hit_tiles, sky_map, precond):
    tiles_dev = sky_map.shape[0]
    pixels = sky_map.shape[2]
    all_tiles = tiles_dev * lax.axis_size(TM)
    position = lax.axis_index(TM)
    local_ids = jnp.mod(hit_tiles[0] - (position - 1) * tiles_dev, all_tiles)
    doubled = 2.0 * pol_angle[0]
    cos_two = jnp.cos(doubled)
    sin_two = jnp.sin(doubled)
    weights = noise_weight[0]
    slot = hit_slot[0]
    pix = tile_pixel[0]
    window = with_halo(as_grid(sky_map), ((TM, 0),), tiles_dev)
    resid, binned = bin_call(local_ids, weights, window, slot, pix, cos_two, sin_two, timestream[0])
    near_tiles = binned.reshape(binned.shape[0], 3, pixels)
    from_upper = passed_along(near_tiles[:tiles_dev], TM, -1)
    from_lower = passed_along(near_tiles[2 * tiles_dev :], TM, 1)
    owned_tiles = near_tiles[tiles_dev : 2 * tiles_dev] + from_upper + from_lower
    grad_share = sum_at_owner(owned_tiles, WAFER, 2)
    share_width = grad_share.shape[2]
    inverse_share = lax.dynamic_slice_in_dim(
        precond, lax.axis_index(WAFER) * share_width, share_width, 2
    )
    dir_share = precondition(grad_share, inverse_share)
    slope_part = jnp.sum(grad_share * dir_share)
    direction = collect(dir_share, WAFER, 2)
    dir_window = with_halo(as_grid(direction), ((TM, 0),), tiles_dev)
    rescanned, parts = scan_call(
        local_ids, weights, slope_part.reshape(1), dir_window, slot, pix, cos_two, sin_two
    )
    totals = summed_by_exchange(parts, WAFER)
    totals = lax.psum(totals, "tm_0")
    totals = summed_by_exchange(totals, ("tm_hi", "tm_lo"))
    step_size = totals[0, 0] / totals[0, 1]
    new_map = sky_map + step_size * direction
    new_residual = (resid - step_size * rescanned)[None]
    return (new_map, new_residual)


def solution(mesh):
    split = Mesh(mesh.devices.reshape(4, 4, 4, 4, 2), TM_WAFER)
    in_specs = (
        P(TM, WAFER, None),
        P(TM, WAFER),
        P(TM, WAFER, None),
        P(TM, WAFER, None),
        P(TM, WAFER, None),
        P(TM, None),
        P(TM, None, None),
        P(TM, None, None),
    )
    out_specs = (P(TM, None, None), P(TM, WAFER, None))
    return jax.shard_map(local, mesh=split, in_specs=in_specs, out_specs=out_specs, check_vma=False)
```

```python
import functools

import jax
import jax.numpy as jnp
from jax import lax
from jax.experimental import pallas as pl
from jax.experimental.pallas import tpu as pltpu
from jax.sharding import Mesh
from jax.sharding import PartitionSpec as P

TM = ("tm_0", "tm_hi", "tm_lo")
WAFER = ("wafer_0", "wafer_1")
TM_WAFER = ("tm_0", "tm_hi", "tm_lo", "wafer_0", "wafer_1")


def with_halo(block, sides, width):
    for axis, dim in sides:
        count = lax.axis_size(axis)
        forward = [(i, i + 1) for i in range(count - 1)]
        forward.append((count - 1, 0))
        backward = [(target, source) for source, target in forward]
        low = lax.ppermute(
            lax.slice_in_dim(block, block.shape[dim] - width, None, axis=dim), axis, forward
        )
        high = lax.ppermute(lax.slice_in_dim(block, 0, width, axis=dim), axis, backward)
        block = jnp.concatenate([low, block, high], axis=dim)
    return block


def passed_along(value, axis, by):
    count = lax.axis_size(axis)
    return lax.ppermute(value, axis, [(i, (i + by) % count) for i in range(count)])


def in_blocks(value, dim, count):
    shape = value.shape
    parts = value.reshape(*shape[:dim], count, shape[dim] // count, *shape[dim + 1 :])
    return jnp.moveaxis(parts, dim, 0)


def sum_at_owner(value, axis, dim):
    count = lax.axis_size(axis)
    parts = lax.all_to_all(in_blocks(value, dim, count), axis, 0, 0, tiled=True)
    return jnp.sum(parts, axis=0)


def laid_out(parts, dim):
    shape = list(parts.shape[1:])
    shape[dim] *= parts.shape[0]
    return jnp.moveaxis(parts, 0, dim).reshape(shape)


def copy_for_each(value, axis):
    copies = jnp.broadcast_to(value, (lax.axis_size(axis), *value.shape))
    return lax.all_to_all(copies, axis, split_axis=0, concat_axis=0, tiled=True)


def collect(value, axis, dim):
    return laid_out(copy_for_each(value, axis), dim)


def summed_by_exchange(value, axis):
    return jnp.sum(copy_for_each(value, axis), axis=0)


def by_axis(value, axes):
    return functools.reduce(lax.psum, axes, value)


def precondition(gradient, inverse):
    g_i = gradient[:, 0]
    g_q = gradient[:, 1]
    g_u = gradient[:, 2]
    out_i = inverse[:, 0] * g_i + inverse[:, 3] * g_q + inverse[:, 4] * g_u
    out_q = inverse[:, 3] * g_i + inverse[:, 1] * g_q + inverse[:, 5] * g_u
    out_u = inverse[:, 4] * g_i + inverse[:, 5] * g_q + inverse[:, 2] * g_u
    return jnp.stack([out_i, out_q, out_u], axis=1)


SIDE = 128


def split2(value):
    hi = value.astype(jnp.bfloat16)
    lo = (value - hi.astype(jnp.float32)).astype(jnp.bfloat16)
    return hi, lo


def row_onehot(slot, pix, rows):
    row = slot * SIDE + jnp.right_shift(pix, 7)
    ids = lax.broadcasted_iota(jnp.int32, (rows, pix.shape[1]), 0)
    return (ids == row).astype(jnp.bfloat16)


def col_mask(pix):
    col = jnp.bitwise_and(pix, SIDE - 1)
    ids = lax.broadcasted_iota(jnp.int32, (SIDE, pix.shape[1]), 0)
    return ids == col


def stacked_map(ids_ref, win_ref, lhs_ref):
    for s in range(ids_ref.shape[0]):
        tile_id = ids_ref[s]
        for comp in range(3):
            hi, lo = split2(win_ref[tile_id, comp].T)
            cols = slice(s * SIDE, (s + 1) * SIDE)
            lhs_ref[comp * SIDE:(comp + 1) * SIDE, cols] = hi
            lhs_ref[(3 + comp) * SIDE:(4 + comp) * SIDE, cols] = lo


def sampled(lhs_ref, at, mask):
    both = jnp.dot(lhs_ref[...], at, preferred_element_type=jnp.float32)
    values = []
    for comp in range(3):
        full = both[comp * SIDE:(comp + 1) * SIDE] + both[(3 + comp) * SIDE:(4 + comp) * SIDE]
        values.append(jnp.sum(jnp.where(mask, full, 0.0), axis=0, keepdims=True))
    return values


def bin_kernel(ids_ref, w_ref, win_ref, slot_ref, pix_ref, cos_ref, sin_ref, ts_ref, resid_ref, g_ref,
               lhs_ref, rhs_ref, acc_ref):
    stacked_map(ids_ref, win_ref, lhs_ref)
    acc_ref[...] = jnp.zeros(acc_ref.shape, jnp.float32)
    rows = lhs_ref.shape[1]
    nt = (((1,), (1,)), ((), ()))

    def body(d, carry):
        slot = slot_ref[pl.ds(d, 1), :]
        pix = pix_ref[pl.ds(d, 1), :]
        cs = cos_ref[pl.ds(d, 1), :]
        sn = sin_ref[pl.ds(d, 1), :]
        at = row_onehot(slot, pix, rows)
        mask = col_mask(pix)
        v0, v1, v2 = sampled(lhs_ref, at, mask)
        resid = ts_ref[pl.ds(d, 1), :] - (v0 + cs * v1 + sn * v2)
        resid_ref[pl.ds(d, 1), :] = resid
        weighted = w_ref[d] * resid
        for comp, term in ((0, weighted), (1, weighted * cs), (2, weighted * sn)):
            hi, lo = split2(jnp.where(mask, term, 0.0))
            rhs_ref[comp * SIDE:(comp + 1) * SIDE, :] = hi
            rhs_ref[(3 + comp) * SIDE:(4 + comp) * SIDE, :] = lo
        acc_ref[...] += lax.dot_general(at, rhs_ref[...], nt, preferred_element_type=jnp.float32)
        return carry

    lax.fori_loop(0, slot_ref.shape[0], body, 0)
    g_ref[...] = jnp.zeros(g_ref.shape, jnp.float32)
    for s in range(ids_ref.shape[0]):
        for comp in range(3):
            rows_s = slice(s * SIDE, (s + 1) * SIDE)
            g_ref[ids_ref[s], comp] = (acc_ref[rows_s, comp * SIDE:(comp + 1) * SIDE]
                              + acc_ref[rows_s, (3 + comp) * SIDE:(4 + comp) * SIDE])


def scan_kernel(ids_ref, w_ref, slope_ref, win_ref, slot_ref, pix_ref, cos_ref, sin_ref, out_ref,
                totals_ref, lhs_ref):
    stacked_map(ids_ref, win_ref, lhs_ref)
    rows = lhs_ref.shape[1]

    def body(d, curve):
        slot = slot_ref[pl.ds(d, 1), :]
        pix = pix_ref[pl.ds(d, 1), :]
        at = row_onehot(slot, pix, rows)
        mask = col_mask(pix)
        v0, v1, v2 = sampled(lhs_ref, at, mask)
        value = v0 + cos_ref[pl.ds(d, 1), :] * v1 + sin_ref[pl.ds(d, 1), :] * v2
        out_ref[pl.ds(d, 1), :] = value
        return curve + w_ref[d] * value * value

    curve = lax.fori_loop(0, slot_ref.shape[0], body, jnp.zeros(cos_ref.shape[1:], jnp.float32)[None])
    curve_sum = jnp.sum(curve, axis=1, keepdims=True)
    lane = lax.broadcasted_iota(jnp.int32, totals_ref.shape, 1)
    totals_ref[...] = jnp.where(lane == 0, slope_ref[0], jnp.where(lane == 1, curve_sum, 0.0))


VMEM = pltpu.MemorySpace.VMEM


def bin_call(local_ids, weights, win, slot, pix, cos_two, sin_two, ts):
    dets, samp = slot.shape
    hits = local_ids.shape[0]
    smem = pl.BlockSpec(memory_space=pltpu.SMEM)
    vmem = pl.BlockSpec(memory_space=VMEM)
    return pl.pallas_call(
        bin_kernel,
        out_shape=(
            jax.ShapeDtypeStruct((dets, samp), jnp.float32),
            jax.ShapeDtypeStruct(win.shape, jnp.float32),
        ),
        in_specs=[smem, smem] + [vmem] * 6,
        out_specs=(vmem, vmem),
        scratch_shapes=[
            pltpu.VMEM((6 * SIDE, hits * SIDE), jnp.bfloat16),
            pltpu.VMEM((6 * SIDE, samp), jnp.bfloat16),
            pltpu.VMEM((hits * SIDE, 6 * SIDE), jnp.float32),
        ],
    )(local_ids, weights, win, slot, pix, cos_two, sin_two, ts)


def scan_call(local_ids, weights, slope, win, slot, pix, cos_two, sin_two):
    hits = local_ids.shape[0]
    smem = pl.BlockSpec(memory_space=pltpu.SMEM)
    vmem = pl.BlockSpec(memory_space=VMEM)
    return pl.pallas_call(
        scan_kernel,
        out_shape=(
            jax.ShapeDtypeStruct(slot.shape, jnp.float32),
            jax.ShapeDtypeStruct((1, SIDE), jnp.float32),
        ),
        in_specs=[smem] * 3 + [vmem] * 5,
        out_specs=(vmem, vmem),
        scratch_shapes=[pltpu.VMEM((6 * SIDE, hits * SIDE), jnp.bfloat16)],
    )(local_ids, weights, slope, win, slot, pix, cos_two, sin_two)


def as_grid(tiles):
    return tiles.reshape(tiles.shape[0], 3, SIDE, SIDE)


def local(timestream, noise_weight, hit_slot, tile_pixel, pol_angle, hit_tiles, sky_map, precond):
    tiles_dev = sky_map.shape[0]
    pixels = sky_map.shape[2]
    all_tiles = tiles_dev * lax.axis_size(TM)
    position = lax.axis_index(TM)
    local_ids = jnp.mod(hit_tiles[0] - (position - 1) * tiles_dev, all_tiles)
    doubled = 2.0 * pol_angle[0]
    cos_two = jnp.cos(doubled)
    sin_two = jnp.sin(doubled)
    weights = noise_weight[0]
    slot = hit_slot[0]
    pix = tile_pixel[0]
    window = with_halo(as_grid(sky_map), ((TM, 0),), tiles_dev)
    resid, binned = bin_call(local_ids, weights, window, slot, pix, cos_two, sin_two, timestream[0])
    near_tiles = binned.reshape(binned.shape[0], 3, pixels)
    from_upper = passed_along(near_tiles[:tiles_dev], TM, -1)
    from_lower = passed_along(near_tiles[2 * tiles_dev :], TM, 1)
    owned_tiles = near_tiles[tiles_dev : 2 * tiles_dev] + from_upper + from_lower
    grad_share = sum_at_owner(owned_tiles, WAFER, 2)
    share_width = grad_share.shape[2]
    inverse_share = lax.dynamic_slice_in_dim(
        precond, lax.axis_index(WAFER) * share_width, share_width, 2
    )
    dir_share = precondition(grad_share, inverse_share)
    slope_part = jnp.sum(grad_share * dir_share)
    direction = collect(dir_share, WAFER, 2)
    dir_window = with_halo(as_grid(direction), ((TM, 0),), tiles_dev)
    rescanned, parts = scan_call(
        local_ids, weights, slope_part.reshape(1), dir_window, slot, pix, cos_two, sin_two
    )
    totals = summed_by_exchange(summed_by_exchange(parts, WAFER), TM)
    step_size = totals[0, 0] / totals[0, 1]
    new_map = sky_map + step_size * direction
    new_residual = (resid - step_size * rescanned)[None]
    return (new_map, new_residual)


def solution(mesh):
    split = Mesh(mesh.devices.reshape(4, 4, 4, 4, 2), TM_WAFER)
    in_specs = (
        P(TM, WAFER, None),
        P(TM, WAFER),
        P(TM, WAFER, None),
        P(TM, WAFER, None),
        P(TM, WAFER, None),
        P(TM, None),
        P(TM, None, None),
        P(TM, None, None),
    )
    out_specs = (P(TM, None, None), P(TM, WAFER, None))
    return jax.shard_map(local, mesh=split, in_specs=in_specs, out_specs=out_specs, check_vma=False)
```

```python
import functools

import jax
import jax.numpy as jnp
from jax import lax
from jax.experimental import pallas as pl
from jax.experimental.pallas import tpu as pltpu
from jax.sharding import Mesh
from jax.sharding import PartitionSpec as P

TM = ("tm_0", "tm_hi", "tm_lo")
WAFER = ("wafer_0", "wafer_1")
TM_WAFER = ("tm_0", "tm_hi", "tm_lo", "wafer_0", "wafer_1")


def with_halo(block, sides, width):
    for axis, dim in sides:
        count = lax.axis_size(axis)
        forward = [(i, i + 1) for i in range(count - 1)]
        forward.append((count - 1, 0))
        backward = [(target, source) for source, target in forward]
        low = lax.ppermute(
            lax.slice_in_dim(block, block.shape[dim] - width, None, axis=dim), axis, forward
        )
        high = lax.ppermute(lax.slice_in_dim(block, 0, width, axis=dim), axis, backward)
        block = jnp.concatenate([low, block, high], axis=dim)
    return block


def passed_along(value, axis, by):
    count = lax.axis_size(axis)
    return lax.ppermute(value, axis, [(i, (i + by) % count) for i in range(count)])


def in_blocks(value, dim, count):
    shape = value.shape
    parts = value.reshape(*shape[:dim], count, shape[dim] // count, *shape[dim + 1 :])
    return jnp.moveaxis(parts, dim, 0)


def sum_at_owner(value, axis, dim):
    count = lax.axis_size(axis)
    parts = lax.all_to_all(in_blocks(value, dim, count), axis, 0, 0, tiled=True)
    return jnp.sum(parts, axis=0)


def laid_out(parts, dim):
    shape = list(parts.shape[1:])
    shape[dim] *= parts.shape[0]
    return jnp.moveaxis(parts, 0, dim).reshape(shape)


def copy_for_each(value, axis):
    copies = jnp.broadcast_to(value, (lax.axis_size(axis), *value.shape))
    return lax.all_to_all(copies, axis, split_axis=0, concat_axis=0, tiled=True)


def collect(value, axis, dim):
    return laid_out(copy_for_each(value, axis), dim)


def summed_by_exchange(value, axis):
    return jnp.sum(copy_for_each(value, axis), axis=0)


def by_axis(value, axes):
    return functools.reduce(lax.psum, axes, value)


def precondition(gradient, inverse):
    g_i = gradient[:, 0]
    g_q = gradient[:, 1]
    g_u = gradient[:, 2]
    out_i = inverse[:, 0] * g_i + inverse[:, 3] * g_q + inverse[:, 4] * g_u
    out_q = inverse[:, 3] * g_i + inverse[:, 1] * g_q + inverse[:, 5] * g_u
    out_u = inverse[:, 4] * g_i + inverse[:, 5] * g_q + inverse[:, 2] * g_u
    return jnp.stack([out_i, out_q, out_u], axis=1)


SIDE = 128


def split2(value):
    hi = value.astype(jnp.bfloat16)
    lo = (value - hi.astype(jnp.float32)).astype(jnp.bfloat16)
    return hi, lo


def row_onehot(slot, pix, rows):
    row = slot * SIDE + jnp.right_shift(pix, 7)
    ids = lax.broadcasted_iota(jnp.int32, (rows, pix.shape[1]), 0)
    return (ids == row).astype(jnp.bfloat16)


def col_mask(pix):
    col = jnp.bitwise_and(pix, SIDE - 1)
    ids = lax.broadcasted_iota(jnp.int32, (SIDE, pix.shape[1]), 0)
    return ids == col


def stacked_map(ids_ref, win_ref, lhs_ref):
    for s in range(ids_ref.shape[0]):
        tile_id = ids_ref[s]
        for comp in range(3):
            hi, lo = split2(win_ref[tile_id, comp].T)
            cols = slice(s * SIDE, (s + 1) * SIDE)
            lhs_ref[comp * SIDE:(comp + 1) * SIDE, cols] = hi
            lhs_ref[(3 + comp) * SIDE:(4 + comp) * SIDE, cols] = lo


def sampled(lhs_ref, at, mask):
    both = jnp.dot(lhs_ref[...], at, preferred_element_type=jnp.float32)
    values = []
    for comp in range(3):
        full = both[comp * SIDE:(comp + 1) * SIDE] + both[(3 + comp) * SIDE:(4 + comp) * SIDE]
        values.append(jnp.sum(jnp.where(mask, full, 0.0), axis=0, keepdims=True))
    return values


def bin_kernel(ids_ref, w_ref, win_ref, slot_ref, pix_ref, cos_ref, sin_ref, ts_ref, resid_ref, g_ref,
               lhs_ref, rhs_ref, acc_ref):
    stacked_map(ids_ref, win_ref, lhs_ref)
    acc_ref[...] = jnp.zeros(acc_ref.shape, jnp.float32)
    rows = lhs_ref.shape[1]
    nt = (((1,), (1,)), ((), ()))

    def body(d, carry):
        slot = slot_ref[pl.ds(d, 1), :]
        pix = pix_ref[pl.ds(d, 1), :]
        cs = cos_ref[pl.ds(d, 1), :]
        sn = sin_ref[pl.ds(d, 1), :]
        at = row_onehot(slot, pix, rows)
        mask = col_mask(pix)
        v0, v1, v2 = sampled(lhs_ref, at, mask)
        resid = ts_ref[pl.ds(d, 1), :] - (v0 + cs * v1 + sn * v2)
        resid_ref[pl.ds(d, 1), :] = resid
        weighted = w_ref[d] * resid
        for comp, term in ((0, weighted), (1, weighted * cs), (2, weighted * sn)):
            hi, lo = split2(jnp.where(mask, term, 0.0))
            rhs_ref[comp * SIDE:(comp + 1) * SIDE, :] = hi
            rhs_ref[(3 + comp) * SIDE:(4 + comp) * SIDE, :] = lo
        acc_ref[...] += lax.dot_general(at, rhs_ref[...], nt, preferred_element_type=jnp.float32)
        return carry

    lax.fori_loop(0, slot_ref.shape[0], body, 0)
    g_ref[...] = jnp.zeros(g_ref.shape, jnp.float32)
    for s in range(ids_ref.shape[0]):
        for comp in range(3):
            rows_s = slice(s * SIDE, (s + 1) * SIDE)
            g_ref[ids_ref[s], comp] = (acc_ref[rows_s, comp * SIDE:(comp + 1) * SIDE]
                              + acc_ref[rows_s, (3 + comp) * SIDE:(4 + comp) * SIDE])


def scan_kernel(ids_ref, w_ref, slope_ref, win_ref, slot_ref, pix_ref, cos_ref, sin_ref, out_ref,
                totals_ref, lhs_ref):
    stacked_map(ids_ref, win_ref, lhs_ref)
    rows = lhs_ref.shape[1]

    def body(d, curve):
        slot = slot_ref[pl.ds(d, 1), :]
        pix = pix_ref[pl.ds(d, 1), :]
        at = row_onehot(slot, pix, rows)
        mask = col_mask(pix)
        v0, v1, v2 = sampled(lhs_ref, at, mask)
        value = v0 + cos_ref[pl.ds(d, 1), :] * v1 + sin_ref[pl.ds(d, 1), :] * v2
        out_ref[pl.ds(d, 1), :] = value
        return curve + w_ref[d] * value * value

    curve = lax.fori_loop(0, slot_ref.shape[0], body, jnp.zeros(cos_ref.shape[1:], jnp.float32)[None])
    curve_sum = jnp.sum(curve, axis=1, keepdims=True)
    lane = lax.broadcasted_iota(jnp.int32, totals_ref.shape, 1)
    totals_ref[...] = jnp.where(lane == 0, slope_ref[0], jnp.where(lane == 1, curve_sum, 0.0))


VMEM = pltpu.MemorySpace.VMEM


def bin_call(local_ids, weights, win, slot, pix, cos_two, sin_two, ts):
    dets, samp = slot.shape
    hits = local_ids.shape[0]
    smem = pl.BlockSpec(memory_space=pltpu.SMEM)
    vmem = pl.BlockSpec(memory_space=VMEM)
    return pl.pallas_call(
        bin_kernel,
        out_shape=(
            jax.ShapeDtypeStruct((dets, samp), jnp.float32),
            jax.ShapeDtypeStruct(win.shape, jnp.float32),
        ),
        in_specs=[smem, smem] + [vmem] * 6,
        out_specs=(vmem, vmem),
        scratch_shapes=[
            pltpu.VMEM((6 * SIDE, hits * SIDE), jnp.bfloat16),
            pltpu.VMEM((6 * SIDE, samp), jnp.bfloat16),
            pltpu.VMEM((hits * SIDE, 6 * SIDE), jnp.float32),
        ],
    )(local_ids, weights, win, slot, pix, cos_two, sin_two, ts)


def scan_call(local_ids, weights, slope, win, slot, pix, cos_two, sin_two):
    hits = local_ids.shape[0]
    smem = pl.BlockSpec(memory_space=pltpu.SMEM)
    vmem = pl.BlockSpec(memory_space=VMEM)
    return pl.pallas_call(
        scan_kernel,
        out_shape=(
            jax.ShapeDtypeStruct(slot.shape, jnp.float32),
            jax.ShapeDtypeStruct((1, SIDE), jnp.float32),
        ),
        in_specs=[smem] * 3 + [vmem] * 5,
        out_specs=(vmem, vmem),
        scratch_shapes=[pltpu.VMEM((6 * SIDE, hits * SIDE), jnp.bfloat16)],
    )(local_ids, weights, slope, win, slot, pix, cos_two, sin_two)


def as_grid(tiles):
    return tiles.reshape(tiles.shape[0], 3, SIDE, SIDE)


def local(timestream, noise_weight, hit_slot, tile_pixel, pol_angle, hit_tiles, sky_map, precond):
    tiles_dev = sky_map.shape[0]
    pixels = sky_map.shape[2]
    all_tiles = tiles_dev * lax.axis_size(TM)
    position = lax.axis_index(TM)
    local_ids = jnp.mod(hit_tiles[0] - (position - 1) * tiles_dev, all_tiles)
    doubled = 2.0 * pol_angle[0]
    cos_two = jnp.cos(doubled)
    sin_two = jnp.sin(doubled)
    weights = noise_weight[0]
    slot = hit_slot[0]
    pix = tile_pixel[0]
    window = with_halo(as_grid(sky_map), ((TM, 0),), tiles_dev)
    resid, binned = bin_call(local_ids, weights, window, slot, pix, cos_two, sin_two, timestream[0])
    near_tiles = binned.reshape(binned.shape[0], 3, pixels)
    wafers = lax.axis_size(WAFER)
    near_blocks = in_blocks(near_tiles, 2, wafers)
    from_upper = passed_along(near_blocks[:, :tiles_dev], TM, -1)
    from_lower = passed_along(near_blocks[:, 2 * tiles_dev :], TM, 1)
    owned_blocks = near_blocks[:, tiles_dev : 2 * tiles_dev] + from_upper + from_lower
    grad_share = jnp.sum(lax.all_to_all(owned_blocks, WAFER, 0, 0, tiled=True), axis=0)
    share_width = grad_share.shape[2]
    inverse_share = lax.dynamic_slice_in_dim(
        precond, lax.axis_index(WAFER) * share_width, share_width, 2
    )
    dir_share = precondition(grad_share, inverse_share)
    slope_part = jnp.sum(grad_share * dir_share)
    direction = collect(dir_share, WAFER, 2)
    dir_window = with_halo(as_grid(direction), ((TM, 0),), tiles_dev)
    rescanned, parts = scan_call(
        local_ids, weights, slope_part.reshape(1), dir_window, slot, pix, cos_two, sin_two
    )
    totals = summed_by_exchange(summed_by_exchange(parts, WAFER), TM)
    step_size = totals[0, 0] / totals[0, 1]
    new_map = sky_map + step_size * direction
    new_residual = (resid - step_size * rescanned)[None]
    return (new_map, new_residual)


def solution(mesh):
    split = Mesh(mesh.devices.reshape(4, 4, 4, 4, 2), TM_WAFER)
    in_specs = (
        P(TM, WAFER, None),
        P(TM, WAFER),
        P(TM, WAFER, None),
        P(TM, WAFER, None),
        P(TM, WAFER, None),
        P(TM, None),
        P(TM, None, None),
        P(TM, None, None),
    )
    out_specs = (P(TM, None, None), P(TM, WAFER, None))
    return jax.shard_map(local, mesh=split, in_specs=in_specs, out_specs=out_specs, check_vma=False)
```

```python
import functools

import jax
import jax.numpy as jnp
from jax import lax
from jax.experimental import pallas as pl
from jax.experimental.pallas import tpu as pltpu
from jax.sharding import Mesh
from jax.sharding import PartitionSpec as P

TM = ("tm_0", "tm_hi", "tm_lo")
WAFER = ("wafer_0", "wafer_1")
TM_WAFER = ("tm_0", "tm_hi", "tm_lo", "wafer_0", "wafer_1")


def with_halo(block, sides, width):
    for axis, dim in sides:
        count = lax.axis_size(axis)
        forward = [(i, i + 1) for i in range(count - 1)]
        forward.append((count - 1, 0))
        backward = [(target, source) for source, target in forward]
        low = lax.ppermute(
            lax.slice_in_dim(block, block.shape[dim] - width, None, axis=dim), axis, forward
        )
        high = lax.ppermute(lax.slice_in_dim(block, 0, width, axis=dim), axis, backward)
        block = jnp.concatenate([low, block, high], axis=dim)
    return block


def passed_along(value, axis, by):
    count = lax.axis_size(axis)
    return lax.ppermute(value, axis, [(i, (i + by) % count) for i in range(count)])


def in_blocks(value, dim, count):
    shape = value.shape
    parts = value.reshape(*shape[:dim], count, shape[dim] // count, *shape[dim + 1 :])
    return jnp.moveaxis(parts, dim, 0)


def sum_at_owner(value, axis, dim):
    count = lax.axis_size(axis)
    parts = lax.all_to_all(in_blocks(value, dim, count), axis, 0, 0, tiled=True)
    return jnp.sum(parts, axis=0)


def laid_out(parts, dim):
    shape = list(parts.shape[1:])
    shape[dim] *= parts.shape[0]
    return jnp.moveaxis(parts, 0, dim).reshape(shape)


def copy_for_each(value, axis):
    copies = jnp.broadcast_to(value, (lax.axis_size(axis), *value.shape))
    return lax.all_to_all(copies, axis, split_axis=0, concat_axis=0, tiled=True)


def collect(value, axis, dim):
    return laid_out(copy_for_each(value, axis), dim)


def summed_by_exchange(value, axis):
    return jnp.sum(copy_for_each(value, axis), axis=0)


def by_axis(value, axes):
    return functools.reduce(lax.psum, axes, value)


def precondition(gradient, inverse):
    g_i = gradient[:, 0]
    g_q = gradient[:, 1]
    g_u = gradient[:, 2]
    out_i = inverse[:, 0] * g_i + inverse[:, 3] * g_q + inverse[:, 4] * g_u
    out_q = inverse[:, 3] * g_i + inverse[:, 1] * g_q + inverse[:, 5] * g_u
    out_u = inverse[:, 4] * g_i + inverse[:, 5] * g_q + inverse[:, 2] * g_u
    return jnp.stack([out_i, out_q, out_u], axis=1)


SIDE = 128


def split2(value):
    hi = value.astype(jnp.bfloat16)
    lo = (value - hi.astype(jnp.float32)).astype(jnp.bfloat16)
    return hi, lo


def row_onehot(slot, pix, rows):
    row = slot * SIDE + jnp.right_shift(pix, 7)
    ids = lax.broadcasted_iota(jnp.int32, (rows, pix.shape[1]), 0)
    return (ids == row).astype(jnp.bfloat16)


def col_mask(pix):
    col = jnp.bitwise_and(pix, SIDE - 1)
    ids = lax.broadcasted_iota(jnp.int32, (SIDE, pix.shape[1]), 0)
    return ids == col


def stacked_map(ids_ref, win_ref, lhs_ref):
    for s in range(ids_ref.shape[0]):
        tile_id = ids_ref[s]
        for comp in range(3):
            hi, lo = split2(win_ref[tile_id, comp].T)
            cols = slice(s * SIDE, (s + 1) * SIDE)
            lhs_ref[comp * SIDE:(comp + 1) * SIDE, cols] = hi
            lhs_ref[(3 + comp) * SIDE:(4 + comp) * SIDE, cols] = lo


def sampled(lhs_ref, at, mask):
    both = jnp.dot(lhs_ref[...], at, preferred_element_type=jnp.float32)
    values = []
    for comp in range(3):
        full = both[comp * SIDE:(comp + 1) * SIDE] + both[(3 + comp) * SIDE:(4 + comp) * SIDE]
        values.append(jnp.sum(jnp.where(mask, full, 0.0), axis=0, keepdims=True))
    return values


def bin_kernel(ids_ref, w_ref, win_ref, slot_ref, pix_ref, cos_ref, sin_ref, ts_ref, resid_ref, g_ref,
               lhs_ref, rhs_ref, acc_ref):
    stacked_map(ids_ref, win_ref, lhs_ref)
    acc_ref[...] = jnp.zeros(acc_ref.shape, jnp.float32)
    rows = lhs_ref.shape[1]
    nt = (((1,), (1,)), ((), ()))

    def body(d, carry):
        slot = slot_ref[pl.ds(d, 1), :]
        pix = pix_ref[pl.ds(d, 1), :]
        cs = cos_ref[pl.ds(d, 1), :]
        sn = sin_ref[pl.ds(d, 1), :]
        at = row_onehot(slot, pix, rows)
        mask = col_mask(pix)
        v0, v1, v2 = sampled(lhs_ref, at, mask)
        resid = ts_ref[pl.ds(d, 1), :] - (v0 + cs * v1 + sn * v2)
        resid_ref[pl.ds(d, 1), :] = resid
        weighted = w_ref[d] * resid
        for comp, term in ((0, weighted), (1, weighted * cs), (2, weighted * sn)):
            hi, lo = split2(jnp.where(mask, term, 0.0))
            rhs_ref[comp * SIDE:(comp + 1) * SIDE, :] = hi
            rhs_ref[(3 + comp) * SIDE:(4 + comp) * SIDE, :] = lo
        acc_ref[...] += lax.dot_general(at, rhs_ref[...], nt, preferred_element_type=jnp.float32)
        return carry

    lax.fori_loop(0, slot_ref.shape[0], body, 0)
    g_ref[...] = jnp.zeros(g_ref.shape, jnp.float32)
    for s in range(ids_ref.shape[0]):
        for comp in range(3):
            rows_s = slice(s * SIDE, (s + 1) * SIDE)
            g_ref[ids_ref[s], comp] = (acc_ref[rows_s, comp * SIDE:(comp + 1) * SIDE]
                              + acc_ref[rows_s, (3 + comp) * SIDE:(4 + comp) * SIDE])


def scan_kernel(ids_ref, w_ref, slope_ref, win_ref, slot_ref, pix_ref, cos_ref, sin_ref, out_ref,
                totals_ref, lhs_ref):
    stacked_map(ids_ref, win_ref, lhs_ref)
    rows = lhs_ref.shape[1]

    def body(d, curve):
        slot = slot_ref[pl.ds(d, 1), :]
        pix = pix_ref[pl.ds(d, 1), :]
        at = row_onehot(slot, pix, rows)
        mask = col_mask(pix)
        v0, v1, v2 = sampled(lhs_ref, at, mask)
        value = v0 + cos_ref[pl.ds(d, 1), :] * v1 + sin_ref[pl.ds(d, 1), :] * v2
        out_ref[pl.ds(d, 1), :] = value
        return curve + w_ref[d] * value * value

    curve = lax.fori_loop(0, slot_ref.shape[0], body, jnp.zeros(cos_ref.shape[1:], jnp.float32)[None])
    curve_sum = jnp.sum(curve, axis=1, keepdims=True)
    lane = lax.broadcasted_iota(jnp.int32, totals_ref.shape, 2)
    totals_ref[...] = jnp.where(lane == 0, slope_ref[0], jnp.where(lane == 1, curve_sum, 0.0))


VMEM = pltpu.MemorySpace.VMEM


def bin_call(local_ids, weights, win, slot, pix, cos_two, sin_two, ts):
    dets, samp = slot.shape
    hits = local_ids.shape[0]
    smem = pl.BlockSpec(memory_space=pltpu.SMEM)
    vmem = pl.BlockSpec(memory_space=VMEM)
    return pl.pallas_call(
        bin_kernel,
        out_shape=(
            jax.ShapeDtypeStruct((dets, samp), jnp.float32),
            jax.ShapeDtypeStruct(win.shape, jnp.float32),
        ),
        in_specs=[smem, smem] + [vmem] * 6,
        out_specs=(vmem, vmem),
        scratch_shapes=[
            pltpu.VMEM((6 * SIDE, hits * SIDE), jnp.bfloat16),
            pltpu.VMEM((6 * SIDE, samp), jnp.bfloat16),
            pltpu.VMEM((hits * SIDE, 6 * SIDE), jnp.float32),
        ],
    )(local_ids, weights, win, slot, pix, cos_two, sin_two, ts)


def scan_call(local_ids, weights, slope, win, slot, pix, cos_two, sin_two, copies):
    hits = local_ids.shape[0]
    smem = pl.BlockSpec(memory_space=pltpu.SMEM)
    vmem = pl.BlockSpec(memory_space=VMEM)
    return pl.pallas_call(
        scan_kernel,
        out_shape=(
            jax.ShapeDtypeStruct(slot.shape, jnp.float32),
            jax.ShapeDtypeStruct((copies, 1, SIDE), jnp.float32),
        ),
        in_specs=[smem] * 3 + [vmem] * 5,
        out_specs=(vmem, vmem),
        scratch_shapes=[pltpu.VMEM((6 * SIDE, hits * SIDE), jnp.bfloat16)],
    )(local_ids, weights, slope, win, slot, pix, cos_two, sin_two)


def as_grid(tiles):
    return tiles.reshape(tiles.shape[0], 3, SIDE, SIDE)


def local(timestream, noise_weight, hit_slot, tile_pixel, pol_angle, hit_tiles, sky_map, precond):
    tiles_dev = sky_map.shape[0]
    pixels = sky_map.shape[2]
    all_tiles = tiles_dev * lax.axis_size(TM)
    position = lax.axis_index(TM)
    local_ids = jnp.mod(hit_tiles[0] - (position - 1) * tiles_dev, all_tiles)
    doubled = 2.0 * pol_angle[0]
    cos_two = jnp.cos(doubled)
    sin_two = jnp.sin(doubled)
    weights = noise_weight[0]
    slot = hit_slot[0]
    pix = tile_pixel[0]
    window = with_halo(as_grid(sky_map), ((TM, 0),), tiles_dev)
    resid, binned = bin_call(local_ids, weights, window, slot, pix, cos_two, sin_two, timestream[0])
    near_tiles = binned.reshape(binned.shape[0], 3, pixels)
    wafers = lax.axis_size(WAFER)
    near_blocks = in_blocks(near_tiles, 2, wafers)
    from_upper = passed_along(near_blocks[:, :tiles_dev], TM, -1)
    from_lower = passed_along(near_blocks[:, 2 * tiles_dev :], TM, 1)
    owned_blocks = near_blocks[:, tiles_dev : 2 * tiles_dev] + from_upper + from_lower
    grad_share = jnp.sum(lax.all_to_all(owned_blocks, WAFER, 0, 0, tiled=True), axis=0)
    share_width = grad_share.shape[2]
    inverse_share = lax.dynamic_slice_in_dim(
        precond, lax.axis_index(WAFER) * share_width, share_width, 2
    )
    dir_share = precondition(grad_share, inverse_share)
    slope_part = jnp.sum(grad_share * dir_share)
    direction = collect(dir_share, WAFER, 2)
    dir_window = with_halo(as_grid(direction), ((TM, 0),), tiles_dev)
    rescanned, parts = scan_call(
        local_ids, weights, slope_part.reshape(1), dir_window, slot, pix, cos_two, sin_two,
        lax.axis_size(WAFER),
    )
    wafer_sum = jnp.sum(lax.all_to_all(parts, WAFER, 0, 0, tiled=True), axis=0)
    totals = summed_by_exchange(wafer_sum, TM)
    step_size = totals[0, 0] / totals[0, 1]
    new_map = sky_map + step_size * direction
    new_residual = (resid - step_size * rescanned)[None]
    return (new_map, new_residual)


def solution(mesh):
    split = Mesh(mesh.devices.reshape(4, 4, 4, 4, 2), TM_WAFER)
    in_specs = (
        P(TM, WAFER, None),
        P(TM, WAFER),
        P(TM, WAFER, None),
        P(TM, WAFER, None),
        P(TM, WAFER, None),
        P(TM, None),
        P(TM, None, None),
        P(TM, None, None),
    )
    out_specs = (P(TM, None, None), P(TM, WAFER, None))
    return jax.shard_map(local, mesh=split, in_specs=in_specs, out_specs=out_specs, check_vma=False)
```
